128 devices in a mesh: gx: 8 (over x_lo, z), gy: 16 (over x_hi, y, core).
Axes of the slice: x: 4 (x_hi: 2, x_lo: 2; x = x_hi * 2 + x_lo), y: 4, z: 4, core: 2. Of those that a mesh axis runs over, the one named last changes fastest.
Arguments:
- queries: bfloat16 [16384, 4096], P(('gx', 'gy')), may hold values from -6 to 6
- new_kv: bfloat16 [16384, 1024], P(('gx', 'gy')), may hold values from -6 to 6
- kv_cache: bfloat16 [4096, 1024], P('gx'), may hold values from -6 to 6
- residual: bfloat16 [16384, 2048], P(('gx', 'gy')), may hold values from -3 to 3
- token_request: int32 [128, 128], P(('gx', 'gy')), may hold values from 0 to 7, never falling along the last dimension, each value on 1 to 32 neighbouring positions
- request_leaf: int32 [128, 8], P(('gx', 'gy')), may hold values from 0 to 15
- mid_parent: int32 [8], replicated, may hold values from 0 to 3
- leaf_parent: int32 [16], replicated, may hold values from 0 to 7
- node_owner: int32 [28], replicated, may hold values from 0 to 7, as said below
- node_len: int32 [28], replicated, may hold values from 1 to 512, as said below
- out_weight: bfloat16 [4096, 2048], P('gy'), may hold values from -0.375 to 0.375
- norm_gain: float32 [2048], replicated, may hold values from 0.1 to 1.9
- route_experts: int32 [16384, 8], P(('gx', 'gy')), may hold values from 0 to 127, all different within a row; in each aligned block of 128 rows (0 to 127, 128 to 255, ...) at most 12 rows name the same one
- route_weights: float32 [16384, 8], P(('gx', 'gy')), may hold values from 0.25 to 2
- expert_gate: bfloat16 [128, 2048, 768], P(('gx', 'gy')), may hold values from -0.125 to 0.125
- expert_up: bfloat16 [128, 2048, 768], P(('gx', 'gy')), may hold values from -0.125 to 0.125
- expert_down: bfloat16 [128, 768, 2048], P(('gx', 'gy')), may hold values from -0.21875 to 0.21875
Outputs:
- layer_out: bfloat16 [16384, 2048], P(('gx', 'gy'))
The draws below stay inside these ranges and needn't reach their ends.
Inputs may be any that keep to these rules, and one draw needn't show every extreme that they name: `token_request`: within one row, requests are numbered from 0 in order; each has 1 to 32 tokens and one has exactly 32. `node_owner`: every owner index holds at least one node; some owner holds exactly one node. `node_len`: the nodes of one owner have lengths that sum to exactly 512; a node that is alone on its owner has 512 rows. `route_experts`: A row's 8 experts differ; in the 128 rows of one device no expert is named more than 12 times, a bound that some block reaches.
All inputs are finite; a program needn't handle non-finite values.
Results may differ from the reference program's by a relative error of at most 0.023.
Values may be sent and summed in bfloat16 or wider, within the bound.
No kernel may reach another device: no remote copies, remote signals or barrier semaphores. Data moves between devices by JAX's collectives and lax.ppermute only.
A program may use at most 128 MiB of HBM per device.

```python
import math
import jax
import jax.numpy as jnp
import numpy as np
from jax import lax

D = 2048
HEADS = 32
KV_HEADS = 4
HEAD_DIM = 128
MOE_FF = 768
TOPK = 8
TOK_DEV = 128
KEY_DEV = 512
ROOTS = 4
MIDS = 8
LEAVES = 16
SUFFIX_MAX = 32
OWNERS = 8
BLOCKS = 128
TOKENS = 16384
KEYS = 4096
EXPERTS = 128
CAP = 12
REQ_DEV = 8
NODES = 28
N_GY = 16


def tree_layout(key):
    base_key = jax.random.fold_in(key, 11)
    perm_key, owner_key, weight_key = jax.random.split(base_key, 3)
    shuffled = jax.random.permutation(perm_key, NODES).astype(jnp.int32)
    spare_owner = jax.random.randint(owner_key, (NODES,), 1, OWNERS, dtype=jnp.int32)
    owner = jnp.where(shuffled < OWNERS, shuffled, spare_owner)
    node_weight = jax.random.randint(weight_key, (NODES,), 1, 9, dtype=jnp.int32)
    same_owner = (owner[:, None] == owner[None, :]).astype(jnp.int32)
    member_count = jnp.sum(same_owner, axis=1)
    weight_total = jnp.sum(same_owner * node_weight[None, :], axis=1)
    base_length = 1 + node_weight * (KEY_DEV - member_count) // weight_total
    filled = jnp.sum(same_owner * base_length[None, :], axis=1)
    labels = jnp.arange(NODES, dtype=jnp.int32)
    later_count = jnp.sum(same_owner * (labels[None, :] > labels[:, None]).astype(jnp.int32), axis=1)
    lengths = base_length + jnp.where(later_count == 0, KEY_DEV - filled, 0)
    return (owner.astype(jnp.int32), lengths.astype(jnp.int32))


def draw_node_owner(key, part):
    return tree_layout(key)[0]


def draw_node_len(key, part):
    return tree_layout(key)[1]


def draw_queries(key, part):
    own_key = jax.random.fold_in(key, 31)
    values = jax.random.truncated_normal(own_key, -5.0, 5.0, (TOKENS, HEADS * HEAD_DIM), jnp.float32)
    return values.astype(jnp.bfloat16)


def draw_new_kv(key, part):
    own_key = jax.random.fold_in(key, 37)
    kv_width = KV_HEADS * HEAD_DIM
    values = jax.random.truncated_normal(own_key, -5.0, 5.0, (TOKENS, 2 * kv_width), jnp.float32)
    return values.astype(jnp.bfloat16)


def set_ends(drawn, stream_key, least, largest):
    longest = drawn.shape.index(max(drawn.shape))
    spots = []
    for shift in (0, 1):
        where = [jax.random.randint(jax.random.fold_in(stream_key, axis), (), 0, length) for axis, length in enumerate(drawn.shape)]
        where[longest] = (where[longest] + shift) % drawn.shape[longest]
        spots.append(tuple(where))
    return drawn.at[spots[0]].set(least).at[spots[1]].set(largest)


def levels(key, dims, cuts, smallest, largest):
    def one(dim, shards_of):
        draws = jax.random.uniform(jax.random.fold_in(jax.random.fold_in(key, 6), dim), (shards_of,), jnp.float32, smallest / len(cuts), largest / len(cuts))
        return jnp.repeat(jnp.exp(draws), dims[dim] // shards_of).reshape((-1,) + (1,) * (len(dims) - dim - 1))

    factor_of = one(*cuts[0])
    for cut in cuts[1:]:
        factor_of = factor_of * one(*cut)
    return factor_of


def length_profile(number_of, total, bound, lean):
    loads = [(1 << 20) // math.isqrt(standing ** lean) + 1 for standing in range(2, number_of + 1)]
    surplus, holding = total - bound - (number_of - 1), [1] * (number_of - 1)
    while surplus > 0:
        candidates = [i for i in range(number_of - 1) if holding[i] < bound]
        whole, budget = sum([loads[i] for i in candidates]), surplus
        for i in candidates:
            extra = min(bound - holding[i], max(1, budget * loads[i] // whole), surplus)
            holding[i] = holding[i] + extra
            surplus = surplus - extra
    return np.array([bound] + holding)


def uneven(stream_key, amount, total, most, slope):
    if amount == 2:
        one = jax.random.randint(stream_key, (), max(1, total - most), min(most, total - 1) + 1)
        return jnp.stack([one, total - one])
    tallies = jnp.asarray(length_profile(amount, total, most, slope), jnp.int32)
    twos = (amount - 1) // 2
    source_of, receiver = tallies[1:1 + 2 * twos:2], tallies[2:2 + 2 * twos:2]
    slack = jnp.minimum(source_of - 1, most - receiver)
    passed = jax.random.randint(jax.random.fold_in(stream_key, 1), (twos,), 0, 1 << 20) % (slack + 1)
    tallies = tallies.at[1:1 + 2 * twos:2].set(source_of - passed).at[2:2 + 2 * twos:2].set(receiver + passed)
    return tallies[jax.random.permutation(jax.random.fold_in(stream_key, 2), amount)]


def assign_block(rng, own, number, rows, amount, top, limit, lean):
    sequence = jax.random.permutation(rng, amount)
    packed, ordinary = shares(amount, rows * top, limit, lean, True), shares(amount, rows * top, limit, lean, False)
    places = jnp.arange(amount)

    def named(sizes, rotation):
        used = int((sizes > 0).sum())
        fixed = max(1, used // 4)
        moved = fixed + (places - fixed + rotation * (used - fixed)) % max(1, amount - fixed)
        return jnp.zeros((amount,), jnp.int32).at[sequence[jnp.where(places < fixed, places, moved)]].set(jnp.asarray(sizes, jnp.int32))

    sizes = jnp.where(number % 4 == 0, named(packed, number // 4), named(ordinary, number - number // 4 - 1))
    mixed = jax.random.permutation(jax.random.fold_in(own, 3), amount)
    donor, receiver = mixed[0:amount // 2 * 2:2], mixed[1:amount // 2 * 2:2]
    room = jnp.minimum(sizes[donor] - 1, limit - sizes[receiver]) // 2
    room = jnp.where((donor == sequence[0]) | (receiver == sequence[0]) | (sizes[receiver] == 0), 0, jnp.maximum(room, 0))
    moved = jax.random.randint(jax.random.fold_in(own, 4), (amount // 2,), 0, 1 << 20) % (room + 1)
    sizes = sizes.at[donor].add(-moved).at[receiver].add(moved)
    items = jnp.searchsorted(jnp.cumsum(sizes), jnp.arange(rows * top), side="right").astype(jnp.int32)
    listing = items.reshape(top, rows).T
    listing = listing[jax.random.permutation(jax.random.fold_in(own, 1), rows)]
    rotation = jax.random.randint(jax.random.fold_in(own, 2), (rows, 1), 0, top)
    return jnp.take_along_axis(listing, (jnp.arange(top)[None, :] + rotation) % top, axis=1)


def shares(amount, total, most, slope, full):
    portions = [(1 << 20) // math.isqrt(grade ** slope) + 1 for grade in range(1, amount + 1)]
    largest = most if full else min(most, max(-(-total // amount), total * portions[0] // sum(portions)))
    least = 1 if total - largest >= amount - 1 else 0
    holding, rest = [largest] + [least] * (amount - 1), total - largest - least * (amount - 1)
    while rest > 0:
        free = [i for i in range(1, amount) if holding[i] < largest] or [i for i in range(1, amount) if holding[i] < most]
        pool, budget = sum([portions[i] for i in free]), rest
        for i in free:
            extra = min(most - holding[i], max(1, budget * portions[i] // pool), rest)
            holding[i] = holding[i] + extra
            rest = rest - extra
    return np.array(holding)


def normal_values(rng, dims, width, limit, cuts=(), kind=jnp.bfloat16):
    result = jax.random.normal(rng, dims, jnp.float32) * width
    if len(cuts) > 0:
        result = levels(rng, dims, cuts, -0.22, 0.18) * result
    return jnp.clip(result, min=-limit, max=limit).astype(kind)


def setup_inputs(seed: int = 0) -> dict:
    key_of = jax.random.split(jax.random.key(seed), 18)
    queries = draw_queries(jax.random.fold_in(key_of[17], 71), 0)
    new_kv = draw_new_kv(jax.random.fold_in(key_of[17], 71), 0)
    kv_cache = normal_values(key_of[2], (KEYS, 2 * KV_HEADS * HEAD_DIM), 1.0, 6.0, ((0, 8),))
    residual = normal_values(key_of[3], (TOKENS, D), 0.5, 3.0, ((0, 128),))
    token_request = jax.vmap(lambda own: jnp.searchsorted(jnp.cumsum(uneven(own, REQ_DEV, TOK_DEV, SUFFIX_MAX, 2)), jnp.arange(TOK_DEV), side="right"))(jax.random.split(key_of[4], BLOCKS)).reshape((BLOCKS, TOK_DEV)).astype(jnp.int32)
    request_leaf = set_ends(jax.random.randint(key_of[5], (BLOCKS, REQ_DEV), 0, LEAVES), jax.random.fold_in(key_of[5], 1), 0, LEAVES - 1).astype(jnp.int32)
    mid_parent = set_ends(jax.random.randint(key_of[6], (MIDS,), 0, ROOTS), jax.random.fold_in(key_of[6], 1), 0, ROOTS - 1).astype(jnp.int32)
    leaf_parent = set_ends(jax.random.randint(key_of[7], (LEAVES,), 0, MIDS), jax.random.fold_in(key_of[7], 1), 0, MIDS - 1).astype(jnp.int32)
    node_owner = draw_node_owner(jax.random.fold_in(key_of[17], 71), 0)
    node_len = draw_node_len(jax.random.fold_in(key_of[17], 71), 0)
    out_weight = normal_values(key_of[10], (HEADS * HEAD_DIM, D), (D // 8) ** -0.5, 0.375, ((0, 16),))
    norm_gain = jnp.clip(1.0 + 0.18 * jax.random.normal(key_of[11], (D,), jnp.float32), 0.1, 1.9)
    route_experts_keys = jax.random.split(jax.random.fold_in(key_of[12], 1), TOKENS // TOK_DEV)
    route_experts_turns = jax.random.permutation(jax.random.fold_in(key_of[12], 3), TOKENS // TOK_DEV)
    route_experts = jax.vmap(lambda own, number: assign_block(jax.random.fold_in(key_of[12], 2), own, number, TOK_DEV, EXPERTS, TOPK, CAP, 2))(route_experts_keys, route_experts_turns).reshape((TOKENS, TOPK))
    route_weights = jnp.clip(jnp.exp(math.log(2.0) - 2.0794415 * jax.random.uniform(key_of[13], (TOKENS, TOPK), jnp.float32) ** levels(key_of[13], (TOKENS, TOPK), ((0, 128),), -0.2, 0.2)), 0.25, 2.0)
    expert_gate = normal_values(key_of[14], (EXPERTS, D, MOE_FF), D ** -0.5, 0.125, ((0, 128),))
    expert_up = normal_values(key_of[15], (EXPERTS, D, MOE_FF), D ** -0.5, 0.125, ((0, 128),))
    expert_down = normal_values(key_of[16], (EXPERTS, MOE_FF, D), MOE_FF ** -0.5, 0.21875, ((0, 128),))
    return {"queries": queries, "new_kv": new_kv, "kv_cache": kv_cache, "residual": residual, "token_request": token_request, "request_leaf": request_leaf, "mid_parent": mid_parent, "leaf_parent": leaf_parent, "node_owner": node_owner, "node_len": node_len, "out_weight": out_weight, "norm_gain": norm_gain, "route_experts": route_experts, "route_weights": route_weights, "expert_gate": expert_gate, "expert_up": expert_up, "expert_down": expert_down}


EPSILON = 1e-06

def node_bounds(node_owner, node_len, span_rows):
    labels = jnp.arange(node_owner.shape[0], dtype=jnp.int32)
    earlier = (node_owner[:, None] == node_owner[None, :]) & (labels[None, :] < labels[:, None])
    before = lax.optimization_barrier(jnp.sum(jnp.where(earlier, node_len[None, :], 0), axis=1)).astype(jnp.int32)
    starts = (node_owner * span_rows + before).astype(jnp.int32)
    return (starts, (starts + node_len).astype(jnp.int32))

def key_labels(first_row, row_count, starts, finish):
    cache_rows = first_row + jnp.arange(row_count, dtype=jnp.int32)
    inside = (cache_rows[:, None] >= starts[None, :]) & (cache_rows[:, None] < finish[None, :])
    labels = jnp.arange(starts.shape[0], dtype=jnp.int32)
    return lax.optimization_barrier(jnp.sum(jnp.where(inside, labels[None, :], 0), axis=1)).astype(jnp.int32)

def path_nodes(requests, leaf_table, mid_parent, leaf_parent):
    picked = requests[:, None] == jnp.arange(leaf_table.shape[0], dtype=jnp.int32)[None, :]
    leaf_node = lax.optimization_barrier(jnp.sum(jnp.where(picked, leaf_table[None, :], 0), axis=1))
    leaf_pick = leaf_node[:, None] == jnp.arange(leaf_parent.shape[0], dtype=jnp.int32)[None, :]
    middle_node = lax.optimization_barrier(jnp.sum(jnp.where(leaf_pick, leaf_parent[None, :], 0), axis=1))
    middle_pick = middle_node[:, None] == jnp.arange(mid_parent.shape[0], dtype=jnp.int32)[None, :]
    root_node = lax.optimization_barrier(jnp.sum(jnp.where(middle_pick, mid_parent[None, :], 0), axis=1))
    return jnp.stack([root_node, ROOTS + middle_node, ROOTS + MIDS + leaf_node], axis=1).astype(jnp.int32)

def reference(queries, new_kv, kv_cache, residual, token_request, request_leaf, mid_parent, leaf_parent, node_owner, node_len, out_weight, norm_gain, route_experts, route_weights, expert_gate, expert_up, expert_down):
    group_size = HEADS // KV_HEADS
    kv_width = KV_HEADS * HEAD_DIM
    head_scale = HEAD_DIM ** (-0.5)
    starts, finish = node_bounds(node_owner, node_len, KEY_DEV)
    labels = key_labels(0, KEYS, starts, finish)
    cache_keys = kv_cache[:, :kv_width].reshape(KEYS, KV_HEADS, HEAD_DIM).astype(jnp.float32)
    cache_values = kv_cache[:, kv_width:].reshape(KEYS, KV_HEADS, HEAD_DIM).astype(jnp.float32)

    def attend(block_inputs):
        query_block, kv_block, requests, leaf_table = block_inputs
        ancestry = path_nodes(requests, leaf_table, mid_parent, leaf_parent)
        query_heads = query_block.reshape(TOK_DEV, KV_HEADS, group_size, HEAD_DIM).astype(jnp.float32)
        new_keys = kv_block[:, :kv_width].reshape(TOK_DEV, KV_HEADS, HEAD_DIM).astype(jnp.float32)
        new_values = kv_block[:, kv_width:].reshape(TOK_DEV, KV_HEADS, HEAD_DIM).astype(jnp.float32)
        positions = jnp.arange(TOK_DEV, dtype=jnp.int32)
        own_mask = (requests[:, None] == requests[None, :]) & (positions[None, :] <= positions[:, None])
        seen_mask = jnp.any(labels[None, :, None] == ancestry[:, None, :], axis=2)
        far_scores = jnp.einsum('tgsd,kgd->gstk', query_heads, cache_keys) * head_scale
        near_scores = jnp.einsum('tgsd,kgd->gstk', query_heads, new_keys) * head_scale
        far_scores = jnp.where(seen_mask[None, None], far_scores, -jnp.inf)
        near_scores = jnp.where(own_mask[None, None], near_scores, -jnp.inf)
        row_max = jnp.maximum(lax.optimization_barrier(jnp.max(far_scores, axis=3)), lax.optimization_barrier(jnp.max(near_scores, axis=3)))
        far_weights = jnp.exp(far_scores - row_max[..., None])
        near_weights = jnp.exp(near_scores - row_max[..., None])
        denominator = lax.optimization_barrier(jnp.sum(far_weights, axis=3)) + lax.optimization_barrier(jnp.sum(near_weights, axis=3))
        far_rounded = lax.optimization_barrier(far_weights.astype(jnp.bfloat16)).astype(jnp.float32)
        near_rounded = lax.optimization_barrier(near_weights.astype(jnp.bfloat16)).astype(jnp.float32)
        numerator = jnp.einsum('gstk,kgd->gstd', far_rounded, cache_values) + jnp.einsum('gstk,kgd->gstd', near_rounded, new_values)
        heads_out = numerator / denominator[..., None]
        return heads_out.transpose(2, 0, 1, 3).reshape(TOK_DEV, HEADS * HEAD_DIM).astype(jnp.bfloat16)
    attended = lax.map(attend, (queries.reshape(BLOCKS, TOK_DEV, HEADS * HEAD_DIM), new_kv.reshape(BLOCKS, TOK_DEV, 2 * kv_width), token_request, request_leaf))
    attended = attended.reshape(TOKENS, HEADS * HEAD_DIM)
    group_rows = HEADS * HEAD_DIM // N_GY
    attended_groups = attended.reshape(TOKENS, N_GY, group_rows)
    weight_groups = out_weight.reshape(N_GY, group_rows, D)

    def add_group(running, position):
        partial_value = jnp.dot(attended_groups[:, position], weight_groups[position], preferred_element_type=jnp.float32)
        partial_value = lax.optimization_barrier(partial_value.astype(jnp.bfloat16)).astype(jnp.float32)
        return (running + partial_value, None)
    projected, _ = lax.scan(add_group, jnp.zeros((TOKENS, D), jnp.float32), jnp.arange(N_GY, dtype=jnp.int32))
    mixed_state = (residual.astype(jnp.float32) + projected).astype(jnp.bfloat16)
    mixed_float = lax.optimization_barrier(mixed_state).astype(jnp.float32)
    normed = (mixed_float * lax.rsqrt(lax.optimization_barrier(jnp.mean(mixed_float * mixed_float, axis=1, keepdims=True)) + EPSILON) * norm_gain.astype(jnp.float32)).astype(jnp.bfloat16)
    flat_experts = route_experts.reshape(BLOCKS, TOK_DEV * TOPK)

    def block_slots(expert_row):
        onehot = (expert_row[:, None] == jnp.arange(EXPERTS, dtype=jnp.int32)[None, :]).astype(jnp.int32)
        return lax.optimization_barrier(jnp.sum((jnp.cumsum(onehot, axis=0) - onehot) * onehot, axis=1)).astype(jnp.int32)
    slot_ids = lax.map(block_slots, flat_experts)
    block_ids = jnp.arange(BLOCKS, dtype=jnp.int32)[:, None]
    target = ((flat_experts * BLOCKS + block_ids) * CAP + slot_ids).reshape(-1)
    slot_table = jnp.full((EXPERTS * BLOCKS * CAP,), -1, jnp.int32).at[target].set(jnp.arange(TOKENS * TOPK, dtype=jnp.int32))
    slot_table = slot_table.reshape(EXPERTS, BLOCKS * CAP)
    weight_flat = route_weights.reshape(-1).astype(jnp.float32)
    normed_float = normed.astype(jnp.float32)

    def expert_step(running, position):
        chosen = slot_table[position]
        is_valid = chosen >= 0
        clipped = jnp.maximum(chosen, 0)
        tokens = clipped // TOPK
        stacked = jnp.where(is_valid[:, None], normed_float[tokens], 0.0)
        gate_act = jnp.dot(stacked, expert_gate[position].astype(jnp.float32), preferred_element_type=jnp.float32)
        up_act = jnp.dot(stacked, expert_up[position].astype(jnp.float32), preferred_element_type=jnp.float32)
        hidden = lax.optimization_barrier((jax.nn.silu(gate_act) * up_act).astype(jnp.bfloat16)).astype(jnp.float32)
        expert_out = jnp.dot(hidden, expert_down[position].astype(jnp.float32), preferred_element_type=jnp.float32)
        expert_out = lax.optimization_barrier(expert_out.astype(jnp.bfloat16)).astype(jnp.float32)
        row_weight = jnp.where(is_valid, weight_flat[clipped], 0.0)
        return (running.at[tokens].add(expert_out * row_weight[:, None]), None)
    routed_sum, _ = lax.scan(expert_step, jnp.zeros((TOKENS, D), jnp.float32), jnp.arange(EXPERTS, dtype=jnp.int32))
    return (mixed_float + routed_sum).astype(jnp.bfloat16)
```

```python
import jax
import jax.numpy as jnp
from jax import lax
from jax.sharding import PartitionSpec as P
from jax.experimental import pallas as pl
from jax.experimental.pallas import tpu as pltpu

HEADS = 32
KV_HEADS = 4
HEAD_DIM = 128
ROOTS = 4
MIDS = 8


EPSILON = 1e-06


def node_bounds(node_owner, node_len, span_rows):
    labels = jnp.arange(node_owner.shape[0], dtype=jnp.int32)
    earlier = (node_owner[:, None] == node_owner[None, :]) & (labels[None, :] < labels[:, None])
    before = jnp.sum(jnp.where(earlier, node_len[None, :], 0), axis=1)
    starts = node_owner * span_rows + before
    return (starts, starts + node_len)


def key_labels(first_row, row_count, starts, finish):
    cache_rows = first_row + jnp.arange(row_count, dtype=jnp.int32)
    inside = (cache_rows[:, None] >= starts[None, :]) & (cache_rows[:, None] < finish[None, :])
    labels = jnp.arange(starts.shape[0], dtype=jnp.int32)
    return jnp.sum(jnp.where(inside, labels[None, :], 0), axis=1)


def path_nodes(requests, leaf_table, mid_parent, leaf_parent):
    picked = requests[:, None] == jnp.arange(leaf_table.shape[0], dtype=jnp.int32)[None, :]
    leaf_node = jnp.sum(jnp.where(picked, leaf_table[None, :], 0), axis=1)
    leaf_pick = leaf_node[:, None] == jnp.arange(leaf_parent.shape[0], dtype=jnp.int32)[None, :]
    middle_node = jnp.sum(jnp.where(leaf_pick, leaf_parent[None, :], 0), axis=1)
    middle_pick = middle_node[:, None] == jnp.arange(mid_parent.shape[0], dtype=jnp.int32)[None, :]
    root_node = jnp.sum(jnp.where(middle_pick, mid_parent[None, :], 0), axis=1)
    return jnp.stack([root_node, ROOTS + middle_node, ROOTS + MIDS + leaf_node], axis=1)


def masked_scores(query_heads, key_rows, allowed, head_scale):
    scores = (
        jnp.einsum("tgsd,kgd->gstk", query_heads, key_rows, preferred_element_type=jnp.float32)
        * head_scale
    )
    return jnp.where(allowed[None, None], scores, -jnp.inf)


def attention_kernel(q_ref, kc_ref, vc_ref, kn_ref, vn_ref, bf_ref, bn_ref, o_ref):
    head_scale = HEAD_DIM ** (-0.5)
    contract = (((1,), (1,)), ((), ()))
    far_keys = kc_ref[...]
    far_values = vc_ref[...]
    near_keys = kn_ref[...]
    near_values = vn_ref[...]
    far_bias = bf_ref[...]
    near_bias = bn_ref[...]
    for head in range(HEADS // KV_HEADS):
        cols = slice(head * HEAD_DIM, (head + 1) * HEAD_DIM)
        query = q_ref[:, cols]
        far = lax.dot_general(query, far_keys, contract, preferred_element_type=jnp.float32) + far_bias
        near = lax.dot_general(query, near_keys, contract, preferred_element_type=jnp.float32) + near_bias
        top = jnp.maximum(jnp.max(far, axis=1, keepdims=True), jnp.max(near, axis=1, keepdims=True))
        far_p = jnp.exp((far - top) * head_scale)
        near_p = jnp.exp((near - top) * head_scale)
        total = jnp.sum(far_p, axis=1, keepdims=True) + jnp.sum(near_p, axis=1, keepdims=True)
        summed = jnp.dot(
            far_p.astype(jnp.bfloat16), far_values, preferred_element_type=jnp.float32
        ) + jnp.dot(near_p.astype(jnp.bfloat16), near_values, preferred_element_type=jnp.float32)
        o_ref[:, cols] = (summed / total).astype(o_ref.dtype)


def tree_attention(queries, cache, new_kv, far_bias, near_bias):
    tokens = queries.shape[0]
    rows = cache.shape[0]
    group_cols = (HEADS // KV_HEADS) * HEAD_DIM
    return pl.pallas_call(
        attention_kernel,
        grid=(KV_HEADS,),
        in_specs=[
            pl.BlockSpec((tokens, group_cols), lambda g: (0, g)),
            pl.BlockSpec((rows, HEAD_DIM), lambda g: (0, g)),
            pl.BlockSpec((rows, HEAD_DIM), lambda g: (0, KV_HEADS + g)),
            pl.BlockSpec((tokens, HEAD_DIM), lambda g: (0, g)),
            pl.BlockSpec((tokens, HEAD_DIM), lambda g: (0, KV_HEADS + g)),
            pl.BlockSpec((tokens, rows), lambda g: (0, 0)),
            pl.BlockSpec((tokens, tokens), lambda g: (0, 0)),
        ],
        out_specs=pl.BlockSpec((tokens, group_cols), lambda g: (0, g)),
        out_shape=jax.ShapeDtypeStruct((tokens, HEADS * HEAD_DIM), jnp.bfloat16),
        compiler_params=pltpu.CompilerParams(vmem_limit_bytes=48 * 1024 * 1024),
    )(queries, cache, cache, new_kv, new_kv, far_bias, near_bias)


def on_device(
    queries,
    new_kv,
    kv_cache,
    residual,
    token_request,
    request_leaf,
    mid_parent,
    leaf_parent,
    node_owner,
    node_len,
    out_weight,
    norm_gain,
    route_experts,
    route_weights,
    expert_gate,
    expert_up,
    expert_down,
):
    tokens_here = queries.shape[0]
    model_width = residual.shape[1]
    group_size = HEADS // KV_HEADS
    kv_width = KV_HEADS * HEAD_DIM
    head_scale = HEAD_DIM ** (-0.5)
    requests = token_request[0]
    ancestry = path_nodes(requests, request_leaf[0], mid_parent, leaf_parent)
    span_rows = kv_cache.shape[0]
    starts, finish = node_bounds(node_owner, node_len, span_rows)
    positions = jnp.arange(tokens_here, dtype=jnp.int32)
    own_mask = (requests[:, None] == requests[None, :]) & (positions[None, :] <= positions[:, None])
    cache_all = lax.all_gather(kv_cache, "gx", axis=0, tiled=True)
    labels = key_labels(0, cache_all.shape[0], starts, finish)
    seen_mask = jnp.any(labels[None, :, None] == ancestry[:, None, :], axis=2)
    far_bias = jnp.where(seen_mask, 0.0, -jnp.inf).astype(jnp.float32)
    near_bias = jnp.where(own_mask, 0.0, -jnp.inf).astype(jnp.float32)
    attended = tree_attention(queries, cache_all, new_kv, far_bias, near_bias)
    shard_rows = out_weight.shape[0]
    shard_piece = lax.all_gather(out_weight, "gy", axis=0, tiled=True)
    block_count = shard_piece.shape[0] // shard_rows
    columns = attended.reshape(tokens_here, block_count, shard_rows)
    partial_value = jnp.einsum(
        "tnr,nrd->ntd",
        columns,
        shard_piece.reshape(block_count, shard_rows, model_width),
        preferred_element_type=jnp.float32,
    )
    partial_value = lax.optimization_barrier(partial_value.astype(jnp.bfloat16))
    projected = jnp.sum(partial_value.astype(jnp.float32), axis=0)
    mixed_state = (residual.astype(jnp.float32) + projected).astype(jnp.bfloat16)
    mixed_float = lax.optimization_barrier(mixed_state).astype(jnp.float32)
    normed = (
        mixed_float
        * lax.rsqrt(jnp.mean(mixed_float * mixed_float, axis=1, keepdims=True) + EPSILON)
        * norm_gain
    ).astype(jnp.bfloat16)
    top_count = route_experts.shape[1]
    expert_count = lax.axis_size("gx") * lax.axis_size("gy") * expert_gate.shape[0]
    capacity = max(2, (3 * tokens_here * top_count + 2 * expert_count - 1) // (2 * expert_count))
    flat_experts = route_experts.reshape(-1)
    onehot = (flat_experts[:, None] == jnp.arange(expert_count, dtype=jnp.int32)[None, :]).astype(
        jnp.int32
    )
    slot_ids = jnp.sum((jnp.cumsum(onehot, axis=0) - onehot) * onehot, axis=1)
    target = flat_experts * capacity + slot_ids
    assignments = tokens_here * top_count
    source = (
        jnp.full((expert_count * capacity,), -1, jnp.int32)
        .at[target]
        .set(jnp.arange(assignments, dtype=jnp.int32))
    )
    is_valid = source >= 0
    source_rows = jnp.maximum(source, 0) // top_count
    outgoing = jnp.where(is_valid[:, None], normed[source_rows], jnp.zeros((), jnp.bfloat16))
    outgoing = outgoing.reshape(expert_count, capacity, model_width)
    arrived = lax.all_to_all(outgoing, ("gx", "gy"), split_axis=0, concat_axis=0, tiled=True)
    stacked = arrived.reshape(-1, model_width)
    gate_act = jnp.dot(stacked, expert_gate[0], preferred_element_type=jnp.float32)
    up_act = jnp.dot(stacked, expert_up[0], preferred_element_type=jnp.float32)
    hidden = (jax.nn.silu(gate_act) * up_act).astype(jnp.bfloat16)
    expert_out = jnp.dot(hidden, expert_down[0], preferred_element_type=jnp.float32).astype(
        jnp.bfloat16
    )
    returned = lax.all_to_all(
        expert_out.reshape(arrived.shape), ("gx", "gy"), split_axis=0, concat_axis=0, tiled=True
    )
    picked_rows = returned.reshape(expert_count * capacity, model_width)[target].reshape(
        tokens_here, top_count, model_width
    )
    routed_sum = jnp.sum(picked_rows.astype(jnp.float32) * route_weights[:, :, None], axis=1)
    return (mixed_float + routed_sum).astype(jnp.bfloat16)


def solution(mesh):
    in_specs = (
        P(("gx", "gy"), None),
        P(("gx", "gy"), None),
        P("gx", None),
        P(("gx", "gy"), None),
        P(("gx", "gy"), None),
        P(("gx", "gy"), None),
        P(),
        P(),
        P(),
        P(),
        P("gy", None),
        P(),
        P(("gx", "gy"), None),
        P(("gx", "gy"), None),
        P(("gx", "gy"), None, None),
        P(("gx", "gy"), None, None),
        P(("gx", "gy"), None, None),
    )
    out_specs = P(("gx", "gy"), None)
    return jax.shard_map(
        on_device, mesh=mesh, in_specs=in_specs, out_specs=out_specs, check_vma=False
    )
```

```python
import jax
import jax.numpy as jnp
from jax import lax
from jax.sharding import PartitionSpec as P
from jax.experimental import pallas as pl
from jax.experimental.pallas import tpu as pltpu

HEADS = 32
KV_HEADS = 4
HEAD_DIM = 128
ROOTS = 4
MIDS = 8


EPSILON = 1e-06


def node_bounds(node_owner, node_len, span_rows):
    labels = jnp.arange(node_owner.shape[0], dtype=jnp.int32)
    earlier = (node_owner[:, None] == node_owner[None, :]) & (labels[None, :] < labels[:, None])
    before = jnp.sum(jnp.where(earlier, node_len[None, :], 0), axis=1)
    starts = node_owner * span_rows + before
    return (starts, starts + node_len)


def key_labels(first_row, row_count, starts, finish):
    cache_rows = first_row + jnp.arange(row_count, dtype=jnp.int32)
    inside = (cache_rows[:, None] >= starts[None, :]) & (cache_rows[:, None] < finish[None, :])
    labels = jnp.arange(starts.shape[0], dtype=jnp.int32)
    return jnp.sum(jnp.where(inside, labels[None, :], 0), axis=1)


def path_nodes(requests, leaf_table, mid_parent, leaf_parent):
    picked = requests[:, None] == jnp.arange(leaf_table.shape[0], dtype=jnp.int32)[None, :]
    leaf_node = jnp.sum(jnp.where(picked, leaf_table[None, :], 0), axis=1)
    leaf_pick = leaf_node[:, None] == jnp.arange(leaf_parent.shape[0], dtype=jnp.int32)[None, :]
    middle_node = jnp.sum(jnp.where(leaf_pick, leaf_parent[None, :], 0), axis=1)
    middle_pick = middle_node[:, None] == jnp.arange(mid_parent.shape[0], dtype=jnp.int32)[None, :]
    root_node = jnp.sum(jnp.where(middle_pick, mid_parent[None, :], 0), axis=1)
    return jnp.stack([root_node, ROOTS + middle_node, ROOTS + MIDS + leaf_node], axis=1)


def masked_scores(query_heads, key_rows, allowed, head_scale):
    scores = (
        jnp.einsum("tgsd,kgd->gstk", query_heads, key_rows, preferred_element_type=jnp.float32)
        * head_scale
    )
    return jnp.where(allowed[None, None], scores, -jnp.inf)


def attention_kernel(q_ref, kc_ref, vc_ref, kn_ref, vn_ref, bf_ref, bn_ref, o_ref):
    head_scale = HEAD_DIM ** (-0.5)
    contract = (((1,), (1,)), ((), ()))
    far_keys = kc_ref[...]
    far_values = vc_ref[...]
    near_keys = kn_ref[...]
    near_values = vn_ref[...]
    far_bias = bf_ref[...]
    near_bias = bn_ref[...]
    for head in range(HEADS // KV_HEADS):
        cols = slice(head * HEAD_DIM, (head + 1) * HEAD_DIM)
        query = q_ref[:, cols]
        far = lax.dot_general(query, far_keys, contract, preferred_element_type=jnp.float32) + far_bias
        near = lax.dot_general(query, near_keys, contract, preferred_element_type=jnp.float32) + near_bias
        top = jnp.maximum(jnp.max(far, axis=1, keepdims=True), jnp.max(near, axis=1, keepdims=True))
        far_p = jnp.exp((far - top) * head_scale)
        near_p = jnp.exp((near - top) * head_scale)
        total = jnp.sum(far_p, axis=1, keepdims=True) + jnp.sum(near_p, axis=1, keepdims=True)
        summed = jnp.dot(
            far_p.astype(jnp.bfloat16), far_values, preferred_element_type=jnp.float32
        ) + jnp.dot(near_p.astype(jnp.bfloat16), near_values, preferred_element_type=jnp.float32)
        o_ref[:, cols] = (summed / total).astype(o_ref.dtype)


def tree_attention(queries, cache, new_kv, far_bias, near_bias):
    tokens = queries.shape[0]
    rows = cache.shape[0]
    group_cols = (HEADS // KV_HEADS) * HEAD_DIM
    return pl.pallas_call(
        attention_kernel,
        grid=(KV_HEADS,),
        in_specs=[
            pl.BlockSpec((tokens, group_cols), lambda g: (0, g)),
            pl.BlockSpec((rows, HEAD_DIM), lambda g: (0, g)),
            pl.BlockSpec((rows, HEAD_DIM), lambda g: (0, KV_HEADS + g)),
            pl.BlockSpec((tokens, HEAD_DIM), lambda g: (0, g)),
            pl.BlockSpec((tokens, HEAD_DIM), lambda g: (0, KV_HEADS + g)),
            pl.BlockSpec((tokens, rows), lambda g: (0, 0)),
            pl.BlockSpec((tokens, tokens), lambda g: (0, 0)),
        ],
        out_specs=pl.BlockSpec((tokens, group_cols), lambda g: (0, g)),
        out_shape=jax.ShapeDtypeStruct((tokens, HEADS * HEAD_DIM), jnp.bfloat16),
        compiler_params=pltpu.CompilerParams(vmem_limit_bytes=48 * 1024 * 1024),
    )(queries, cache, cache, new_kv, new_kv, far_bias, near_bias)


def on_device(
    queries,
    new_kv,
    kv_cache,
    residual,
    token_request,
    request_leaf,
    mid_parent,
    leaf_parent,
    node_owner,
    node_len,
    out_weight,
    norm_gain,
    route_experts,
    route_weights,
    expert_gate,
    expert_up,
    expert_down,
):
    tokens_here = queries.shape[0]
    model_width = residual.shape[1]
    group_size = HEADS // KV_HEADS
    kv_width = KV_HEADS * HEAD_DIM
    head_scale = HEAD_DIM ** (-0.5)
    requests = token_request[0]
    ancestry = path_nodes(requests, request_leaf[0], mid_parent, leaf_parent)
    span_rows = kv_cache.shape[0]
    starts, finish = node_bounds(node_owner, node_len, span_rows)
    positions = jnp.arange(tokens_here, dtype=jnp.int32)
    own_mask = (requests[:, None] == requests[None, :]) & (positions[None, :] <= positions[:, None])
    cache_all = lax.all_gather(kv_cache, "gx", axis=0, tiled=True)
    labels = key_labels(0, cache_all.shape[0], starts, finish)
    seen_mask = jnp.any(labels[None, :, None] == ancestry[:, None, :], axis=2)
    far_bias = jnp.where(seen_mask, 0.0, -jnp.inf).astype(jnp.float32)
    near_bias = jnp.where(own_mask, 0.0, -jnp.inf).astype(jnp.float32)
    attended = tree_attention(queries, cache_all, new_kv, far_bias, near_bias)
    shard_rows = out_weight.shape[0]
    shard_piece = lax.all_gather(out_weight, "gy", axis=0, tiled=True)
    block_count = shard_piece.shape[0] // shard_rows
    columns = attended.reshape(tokens_here, block_count, shard_rows)
    partial_value = jnp.einsum(
        "tnr,nrd->ntd",
        columns,
        shard_piece.reshape(block_count, shard_rows, model_width),
        preferred_element_type=jnp.float32,
    )
    partial_value = lax.optimization_barrier(partial_value.astype(jnp.bfloat16))
    projected = jnp.sum(partial_value.astype(jnp.float32), axis=0)
    mixed_state = (residual.astype(jnp.float32) + projected).astype(jnp.bfloat16)
    mixed_float = lax.optimization_barrier(mixed_state).astype(jnp.float32)
    normed = (
        mixed_float
        * lax.rsqrt(jnp.mean(mixed_float * mixed_float, axis=1, keepdims=True) + EPSILON)
        * norm_gain
    ).astype(jnp.bfloat16)
    top_count = route_experts.shape[1]
    expert_count = lax.axis_size("gx") * lax.axis_size("gy") * expert_gate.shape[0]
    capacity = max(2, (3 * tokens_here * top_count + 2 * expert_count - 1) // (2 * expert_count))
    flat_experts = route_experts.reshape(-1)
    onehot = (flat_experts[:, None] == jnp.arange(expert_count, dtype=jnp.int32)[None, :]).astype(
        jnp.int32
    )
    slot_ids = jnp.sum((jnp.cumsum(onehot, axis=0) - onehot) * onehot, axis=1)
    slot_ids = slot_ids.reshape(tokens_here, top_count)
    slot_range = jnp.arange(capacity, dtype=jnp.int32)[:, None, None, None]
    expert_range = jnp.arange(expert_count, dtype=jnp.int32)[None, None, :, None]
    match = (slot_ids[None, :, None, :] == slot_range) & (route_experts[None, :, None, :] == expert_range)
    pick = jnp.any(match, axis=3).astype(jnp.bfloat16)
    weight_pick = jnp.sum(jnp.where(match, route_weights[None, :, None, :], 0.0), axis=3)
    outgoing = jnp.concatenate(
        [
            jnp.dot(pick[slot].T, normed, preferred_element_type=jnp.float32).astype(jnp.bfloat16)
            for slot in range(capacity)
        ],
        axis=1,
    )
    arrived = lax.all_to_all(outgoing, ("gx", "gy"), split_axis=0, concat_axis=0, tiled=True)
    stacked = jnp.concatenate(
        [arrived[:, slot * model_width : (slot + 1) * model_width] for slot in range(capacity)], axis=0
    )
    gate_act = jnp.dot(stacked, expert_gate[0], preferred_element_type=jnp.float32)
    up_act = jnp.dot(stacked, expert_up[0], preferred_element_type=jnp.float32)
    hidden = (jax.nn.silu(gate_act) * up_act).astype(jnp.bfloat16)
    expert_out = jnp.dot(hidden, expert_down[0], preferred_element_type=jnp.float32).astype(
        jnp.bfloat16
    )
    sources = arrived.shape[0]
    backward = jnp.concatenate(
        [expert_out[slot * sources : (slot + 1) * sources] for slot in range(capacity)], axis=1
    )
    returned = lax.all_to_all(backward, ("gx", "gy"), split_axis=0, concat_axis=0, tiled=True)
    routed_sum = mixed_float
    for slot in range(capacity):
        routed_sum = routed_sum + jnp.dot(
            weight_pick[slot],
            returned[:, slot * model_width : (slot + 1) * model_width].astype(jnp.float32),
            precision=lax.Precision.HIGHEST,
            preferred_element_type=jnp.float32,
        )
    return routed_sum.astype(jnp.bfloat16)

def solution(mesh):
    in_specs = (
        P(("gx", "gy"), None),
        P(("gx", "gy"), None),
        P("gx", None),
        P(("gx", "gy"), None),
        P(("gx", "gy"), None),
        P(("gx", "gy"), None),
        P(),
        P(),
        P(),
        P(),
        P("gy", None),
        P(),
        P(("gx", "gy"), None),
        P(("gx", "gy"), None),
        P(("gx", "gy"), None, None),
        P(("gx", "gy"), None, None),
        P(("gx", "gy"), None, None),
    )
    out_specs = P(("gx", "gy"), None)
    return jax.shard_map(
        on_device, mesh=mesh, in_specs=in_specs, out_specs=out_specs, check_vma=False
    )
```

```python
import jax
import jax.numpy as jnp
from jax import lax
from jax.sharding import PartitionSpec as P
from jax.experimental import pallas as pl
from jax.experimental.pallas import tpu as pltpu

HEADS = 32
KV_HEADS = 4
HEAD_DIM = 128
ROOTS = 4
MIDS = 8


EPSILON = 1e-06


def node_bounds(node_owner, node_len, span_rows):
    labels = jnp.arange(node_owner.shape[0], dtype=jnp.int32)
    earlier = (node_owner[:, None] == node_owner[None, :]) & (labels[None, :] < labels[:, None])
    before = jnp.sum(jnp.where(earlier, node_len[None, :], 0), axis=1)
    starts = node_owner * span_rows + before
    return (starts, starts + node_len)


def key_labels(first_row, row_count, starts, finish):
    cache_rows = first_row + jnp.arange(row_count, dtype=jnp.int32)
    inside = (cache_rows[:, None] >= starts[None, :]) & (cache_rows[:, None] < finish[None, :])
    labels = jnp.arange(starts.shape[0], dtype=jnp.int32)
    return jnp.sum(jnp.where(inside, labels[None, :], 0), axis=1)


def path_nodes(requests, leaf_table, mid_parent, leaf_parent):
    picked = requests[:, None] == jnp.arange(leaf_table.shape[0], dtype=jnp.int32)[None, :]
    leaf_node = jnp.sum(jnp.where(picked, leaf_table[None, :], 0), axis=1)
    leaf_pick = leaf_node[:, None] == jnp.arange(leaf_parent.shape[0], dtype=jnp.int32)[None, :]
    middle_node = jnp.sum(jnp.where(leaf_pick, leaf_parent[None, :], 0), axis=1)
    middle_pick = middle_node[:, None] == jnp.arange(mid_parent.shape[0], dtype=jnp.int32)[None, :]
    root_node = jnp.sum(jnp.where(middle_pick, mid_parent[None, :], 0), axis=1)
    return jnp.stack([root_node, ROOTS + middle_node, ROOTS + MIDS + leaf_node], axis=1)


def masked_scores(query_heads, key_rows, allowed, head_scale):
    scores = (
        jnp.einsum("tgsd,kgd->gstk", query_heads, key_rows, preferred_element_type=jnp.float32)
        * head_scale
    )
    return jnp.where(allowed[None, None], scores, -jnp.inf)


def attention_kernel(q_ref, kc_ref, vc_ref, kn_ref, vn_ref, bf_ref, bn_ref, o_ref):
    head_scale = HEAD_DIM ** (-0.5)
    contract = (((1,), (1,)), ((), ()))
    far_keys = kc_ref[...]
    far_values = vc_ref[...]
    near_keys = kn_ref[...]
    near_values = vn_ref[...]
    far_bias = bf_ref[...]
    near_bias = bn_ref[...]
    for head in range(HEADS // KV_HEADS):
        cols = slice(head * HEAD_DIM, (head + 1) * HEAD_DIM)
        query = q_ref[:, cols]
        far = lax.dot_general(query, far_keys, contract, preferred_element_type=jnp.float32) + far_bias
        near = lax.dot_general(query, near_keys, contract, preferred_element_type=jnp.float32) + near_bias
        top = jnp.maximum(jnp.max(far, axis=1, keepdims=True), jnp.max(near, axis=1, keepdims=True))
        far_p = jnp.exp((far - top) * head_scale)
        near_p = jnp.exp((near - top) * head_scale)
        total = jnp.sum(far_p, axis=1, keepdims=True) + jnp.sum(near_p, axis=1, keepdims=True)
        summed = jnp.dot(
            far_p.astype(jnp.bfloat16), far_values, preferred_element_type=jnp.float32
        ) + jnp.dot(near_p.astype(jnp.bfloat16), near_values, preferred_element_type=jnp.float32)
        o_ref[:, cols] = (summed / total).astype(o_ref.dtype)


def tree_attention(queries, cache, new_kv, far_bias, near_bias):
    tokens = queries.shape[0]
    rows = cache.shape[0]
    group_cols = (HEADS // KV_HEADS) * HEAD_DIM
    return pl.pallas_call(
        attention_kernel,
        grid=(KV_HEADS,),
        in_specs=[
            pl.BlockSpec((tokens, group_cols), lambda g: (0, g)),
            pl.BlockSpec((rows, HEAD_DIM), lambda g: (0, g)),
            pl.BlockSpec((rows, HEAD_DIM), lambda g: (0, KV_HEADS + g)),
            pl.BlockSpec((tokens, HEAD_DIM), lambda g: (0, g)),
            pl.BlockSpec((tokens, HEAD_DIM), lambda g: (0, KV_HEADS + g)),
            pl.BlockSpec((tokens, rows), lambda g: (0, 0)),
            pl.BlockSpec((tokens, tokens), lambda g: (0, 0)),
        ],
        out_specs=pl.BlockSpec((tokens, group_cols), lambda g: (0, g)),
        out_shape=jax.ShapeDtypeStruct((tokens, HEADS * HEAD_DIM), jnp.bfloat16),
        compiler_params=pltpu.CompilerParams(vmem_limit_bytes=48 * 1024 * 1024),
    )(queries, cache, cache, new_kv, new_kv, far_bias, near_bias)


def on_device(
    queries,
    new_kv,
    kv_cache,
    residual,
    token_request,
    request_leaf,
    mid_parent,
    leaf_parent,
    node_owner,
    node_len,
    out_weight,
    norm_gain,
    route_experts,
    route_weights,
    expert_gate,
    expert_up,
    expert_down,
):
    tokens_here = queries.shape[0]
    model_width = residual.shape[1]
    group_size = HEADS // KV_HEADS
    kv_width = KV_HEADS * HEAD_DIM
    head_scale = HEAD_DIM ** (-0.5)
    requests = token_request[0]
    ancestry = path_nodes(requests, request_leaf[0], mid_parent, leaf_parent)
    span_rows = kv_cache.shape[0]
    starts, finish = node_bounds(node_owner, node_len, span_rows)
    positions = jnp.arange(tokens_here, dtype=jnp.int32)
    own_mask = (requests[:, None] == requests[None, :]) & (positions[None, :] <= positions[:, None])
    cache_all = lax.all_gather(kv_cache, "gx", axis=0, tiled=True)
    labels = key_labels(0, cache_all.shape[0], starts, finish)
    seen_mask = jnp.any(labels[None, :, None] == ancestry[:, None, :], axis=2)
    far_bias = jnp.where(seen_mask, 0.0, -jnp.inf).astype(jnp.float32)
    near_bias = jnp.where(own_mask, 0.0, -jnp.inf).astype(jnp.float32)
    attended = tree_attention(queries, cache_all, new_kv, far_bias, near_bias)
    shard_rows = out_weight.shape[0]
    shard_piece = lax.all_gather(out_weight, "gy", axis=0, tiled=True)
    block_count = shard_piece.shape[0] // shard_rows
    columns = attended.reshape(tokens_here, block_count, shard_rows)
    partial_value = jnp.einsum(
        "tnr,nrd->ntd",
        columns,
        shard_piece.reshape(block_count, shard_rows, model_width),
        preferred_element_type=jnp.float32,
    )
    partial_value = lax.optimization_barrier(partial_value.astype(jnp.bfloat16))
    projected = jnp.sum(partial_value.astype(jnp.float32), axis=0)
    mixed_state = (residual.astype(jnp.float32) + projected).astype(jnp.bfloat16)
    mixed_float = lax.optimization_barrier(mixed_state).astype(jnp.float32)
    normed = (
        mixed_float
        * lax.rsqrt(jnp.mean(mixed_float * mixed_float, axis=1, keepdims=True) + EPSILON)
        * norm_gain
    ).astype(jnp.bfloat16)
    top_count = route_experts.shape[1]
    expert_count = lax.axis_size("gx") * lax.axis_size("gy") * expert_gate.shape[0]
    capacity = max(2, (3 * tokens_here * top_count + 2 * expert_count - 1) // (2 * expert_count))
    slots = -(-capacity // 16) * 16
    flat_experts = route_experts.reshape(-1)
    onehot = (flat_experts[:, None] == jnp.arange(expert_count, dtype=jnp.int32)[None, :]).astype(
        jnp.int32
    )
    slot_ids = jnp.sum((jnp.cumsum(onehot, axis=0) - onehot) * onehot, axis=1)
    target = (flat_experts * slots + slot_ids).reshape(tokens_here, top_count)
    row_range = jnp.arange(expert_count * slots, dtype=jnp.int32)
    pick = jnp.any(target[None, :, :] == row_range[:, None, None], axis=2).astype(jnp.bfloat16)
    weight_pick = jnp.sum(
        jnp.where(target[:, None, :] == row_range[None, :, None], route_weights[:, None, :], 0.0),
        axis=2,
    )
    outgoing = jnp.dot(pick, normed, preferred_element_type=jnp.float32).astype(jnp.bfloat16)
    outgoing = outgoing.reshape(expert_count, slots, model_width)
    arrived = lax.all_to_all(outgoing, ("gx", "gy"), split_axis=0, concat_axis=0, tiled=True)
    stacked = arrived.reshape(-1, model_width)
    gate_act = jnp.dot(stacked, expert_gate[0], preferred_element_type=jnp.float32)
    up_act = jnp.dot(stacked, expert_up[0], preferred_element_type=jnp.float32)
    hidden = (jax.nn.silu(gate_act) * up_act).astype(jnp.bfloat16)
    expert_out = jnp.dot(hidden, expert_down[0], preferred_element_type=jnp.float32).astype(
        jnp.bfloat16
    )
    returned = lax.all_to_all(
        expert_out.reshape(arrived.shape), ("gx", "gy"), split_axis=0, concat_axis=0, tiled=True
    )
    routed_sum = jnp.dot(
        weight_pick,
        returned.reshape(-1, model_width).astype(jnp.float32),
        precision=lax.Precision.HIGHEST,
        preferred_element_type=jnp.float32,
    )
    return (mixed_float + routed_sum).astype(jnp.bfloat16)

def solution(mesh):
    in_specs = (
        P(("gx", "gy"), None),
        P(("gx", "gy"), None),
        P("gx", None),
        P(("gx", "gy"), None),
        P(("gx", "gy"), None),
        P(("gx", "gy"), None),
        P(),
        P(),
        P(),
        P(),
        P("gy", None),
        P(),
        P(("gx", "gy"), None),
        P(("gx", "gy"), None),
        P(("gx", "gy"), None, None),
        P(("gx", "gy"), None, None),
        P(("gx", "gy"), None, None),
    )
    out_specs = P(("gx", "gy"), None)
    return jax.shard_map(
        on_device, mesh=mesh, in_specs=in_specs, out_specs=out_specs, check_vma=False
    )
```

```python
import jax
import jax.numpy as jnp
from jax import lax
from jax.sharding import PartitionSpec as P
from jax.experimental import pallas as pl
from jax.experimental.pallas import tpu as pltpu

HEADS = 32
KV_HEADS = 4
HEAD_DIM = 128
ROOTS = 4
MIDS = 8


EPSILON = 1e-06


def node_bounds(node_owner, node_len, span_rows):
    labels = jnp.arange(node_owner.shape[0], dtype=jnp.int32)
    earlier = (node_owner[:, None] == node_owner[None, :]) & (labels[None, :] < labels[:, None])
    before = jnp.sum(jnp.where(earlier, node_len[None, :], 0), axis=1)
    starts = node_owner * span_rows + before
    return (starts, starts + node_len)


def key_labels(first_row, row_count, starts, finish):
    cache_rows = first_row + jnp.arange(row_count, dtype=jnp.int32)
    inside = (cache_rows[:, None] >= starts[None, :]) & (cache_rows[:, None] < finish[None, :])
    labels = jnp.arange(starts.shape[0], dtype=jnp.int32)
    return jnp.sum(jnp.where(inside, labels[None, :], 0), axis=1)


def path_nodes(requests, leaf_table, mid_parent, leaf_parent):
    picked = requests[:, None] == jnp.arange(leaf_table.shape[0], dtype=jnp.int32)[None, :]
    leaf_node = jnp.sum(jnp.where(picked, leaf_table[None, :], 0), axis=1)
    leaf_pick = leaf_node[:, None] == jnp.arange(leaf_parent.shape[0], dtype=jnp.int32)[None, :]
    middle_node = jnp.sum(jnp.where(leaf_pick, leaf_parent[None, :], 0), axis=1)
    middle_pick = middle_node[:, None] == jnp.arange(mid_parent.shape[0], dtype=jnp.int32)[None, :]
    root_node = jnp.sum(jnp.where(middle_pick, mid_parent[None, :], 0), axis=1)
    return jnp.stack([root_node, ROOTS + middle_node, ROOTS + MIDS + leaf_node], axis=1)


def masked_scores(query_heads, key_rows, allowed, head_scale):
    scores = (
        jnp.einsum("tgsd,kgd->gstk", query_heads, key_rows, preferred_element_type=jnp.float32)
        * head_scale
    )
    return jnp.where(allowed[None, None], scores, -jnp.inf)


def attention_kernel(q_ref, kc_ref, vc_ref, kn_ref, vn_ref, bf_ref, bn_ref, o_ref):
    head_scale = HEAD_DIM ** (-0.5)
    contract = (((1,), (1,)), ((), ()))
    far_keys = kc_ref[...]
    far_values = vc_ref[...]
    near_keys = kn_ref[...]
    near_values = vn_ref[...]
    far_bias = bf_ref[...]
    near_bias = bn_ref[...]
    for head in range(HEADS // KV_HEADS):
        cols = slice(head * HEAD_DIM, (head + 1) * HEAD_DIM)
        query = q_ref[:, cols]
        far = lax.dot_general(query, far_keys, contract, preferred_element_type=jnp.float32) + far_bias
        near = lax.dot_general(query, near_keys, contract, preferred_element_type=jnp.float32) + near_bias
        top = jnp.maximum(jnp.max(far, axis=1, keepdims=True), jnp.max(near, axis=1, keepdims=True))
        far_p = jnp.exp((far - top) * head_scale)
        near_p = jnp.exp((near - top) * head_scale)
        total = jnp.sum(far_p, axis=1, keepdims=True) + jnp.sum(near_p, axis=1, keepdims=True)
        summed = jnp.dot(
            far_p.astype(jnp.bfloat16), far_values, preferred_element_type=jnp.float32
        ) + jnp.dot(near_p.astype(jnp.bfloat16), near_values, preferred_element_type=jnp.float32)
        o_ref[:, cols] = (summed / total).astype(o_ref.dtype)


def tree_attention(queries, cache, new_kv, far_bias, near_bias):
    tokens = queries.shape[0]
    rows = cache.shape[0]
    group_cols = (HEADS // KV_HEADS) * HEAD_DIM
    return pl.pallas_call(
        attention_kernel,
        grid=(KV_HEADS,),
        in_specs=[
            pl.BlockSpec((tokens, group_cols), lambda g: (0, g)),
            pl.BlockSpec((rows, HEAD_DIM), lambda g: (0, g)),
            pl.BlockSpec((rows, HEAD_DIM), lambda g: (0, KV_HEADS + g)),
            pl.BlockSpec((tokens, HEAD_DIM), lambda g: (0, g)),
            pl.BlockSpec((tokens, HEAD_DIM), lambda g: (0, KV_HEADS + g)),
            pl.BlockSpec((tokens, rows), lambda g: (0, 0)),
            pl.BlockSpec((tokens, tokens), lambda g: (0, 0)),
        ],
        out_specs=pl.BlockSpec((tokens, group_cols), lambda g: (0, g)),
        out_shape=jax.ShapeDtypeStruct((tokens, HEADS * HEAD_DIM), jnp.bfloat16),
        compiler_params=pltpu.CompilerParams(vmem_limit_bytes=48 * 1024 * 1024),
    )(queries, cache, cache, new_kv, new_kv, far_bias, near_bias)


def on_device(
    queries,
    new_kv,
    kv_cache,
    residual,
    token_request,
    request_leaf,
    mid_parent,
    leaf_parent,
    node_owner,
    node_len,
    out_weight,
    norm_gain,
    route_experts,
    route_weights,
    expert_gate,
    expert_up,
    expert_down,
):
    tokens_here = queries.shape[0]
    model_width = residual.shape[1]
    group_size = HEADS // KV_HEADS
    kv_width = KV_HEADS * HEAD_DIM
    head_scale = HEAD_DIM ** (-0.5)
    requests = token_request[0]
    ancestry = path_nodes(requests, request_leaf[0], mid_parent, leaf_parent)
    span_rows = kv_cache.shape[0]
    starts, finish = node_bounds(node_owner, node_len, span_rows)
    positions = jnp.arange(tokens_here, dtype=jnp.int32)
    own_mask = (requests[:, None] == requests[None, :]) & (positions[None, :] <= positions[:, None])
    cache_all = lax.all_gather(kv_cache, "gx", axis=0, tiled=True)
    labels = key_labels(0, cache_all.shape[0], starts, finish)
    seen_mask = jnp.any(labels[None, :, None] == ancestry[:, None, :], axis=2)
    far_bias = jnp.where(seen_mask, 0.0, -jnp.inf).astype(jnp.float32)
    near_bias = jnp.where(own_mask, 0.0, -jnp.inf).astype(jnp.float32)
    attended = tree_attention(queries, cache_all, new_kv, far_bias, near_bias)
    shard_rows = out_weight.shape[0]
    core = lax.axis_index("core")
    swap = [(0, 1), (1, 0)]
    parity_rows = lax.all_gather(out_weight, "gyo", axis=0, tiled=False)
    partner = lax.ppermute(attended, "core", swap)
    pair = jnp.concatenate([attended, partner], axis=0)
    columns = jnp.stack(
        [
            lax.dynamic_slice_in_dim(pair, (2 * group + core) * shard_rows, shard_rows, axis=1)
            for group in range(parity_rows.shape[0])
        ],
        axis=1,
    )
    partial_value = jnp.einsum(
        "tnr,nrd->ntd", columns, parity_rows, preferred_element_type=jnp.float32
    )
    partial_value = lax.optimization_barrier(partial_value.astype(jnp.bfloat16))
    pair_sum = jnp.sum(partial_value.astype(jnp.float32), axis=0)
    projected = pair_sum[:tokens_here] + lax.ppermute(pair_sum[tokens_here:], "core", swap)
    mixed_state = (residual.astype(jnp.float32) + projected).astype(jnp.bfloat16)
    mixed_float = lax.optimization_barrier(mixed_state).astype(jnp.float32)
    normed = (
        mixed_float
        * lax.rsqrt(jnp.mean(mixed_float * mixed_float, axis=1, keepdims=True) + EPSILON)
        * norm_gain
    ).astype(jnp.bfloat16)
    top_count = route_experts.shape[1]
    expert_count = lax.axis_size("gx") * lax.axis_size("gyo") * lax.axis_size("core") * expert_gate.shape[0]
    capacity = max(2, (3 * tokens_here * top_count + 2 * expert_count - 1) // (2 * expert_count))
    slots = -(-capacity // 16) * 16
    flat_experts = route_experts.reshape(-1)
    onehot = (flat_experts[:, None] == jnp.arange(expert_count, dtype=jnp.int32)[None, :]).astype(
        jnp.int32
    )
    slot_ids = jnp.sum((jnp.cumsum(onehot, axis=0) - onehot) * onehot, axis=1)
    target = (flat_experts * slots + slot_ids).reshape(tokens_here, top_count)
    row_range = jnp.arange(expert_count * slots, dtype=jnp.int32)
    pick = jnp.any(target[None, :, :] == row_range[:, None, None], axis=2).astype(jnp.bfloat16)
    weight_pick = jnp.sum(
        jnp.where(target[:, None, :] == row_range[None, :, None], route_weights[:, None, :], 0.0),
        axis=2,
    )
    outgoing = jnp.dot(pick, normed, preferred_element_type=jnp.float32).astype(jnp.bfloat16)
    outgoing = outgoing.reshape(expert_count, slots, model_width)
    arrived = lax.all_to_all(outgoing, TOKEN_AXES, split_axis=0, concat_axis=0, tiled=True)
    stacked = arrived.reshape(-1, model_width)
    gate_act = jnp.dot(stacked, expert_gate[0], preferred_element_type=jnp.float32)
    up_act = jnp.dot(stacked, expert_up[0], preferred_element_type=jnp.float32)
    hidden = (jax.nn.silu(gate_act) * up_act).astype(jnp.bfloat16)
    expert_out = jnp.dot(hidden, expert_down[0], preferred_element_type=jnp.float32).astype(
        jnp.bfloat16
    )
    returned = lax.all_to_all(
        expert_out.reshape(arrived.shape), TOKEN_AXES, split_axis=0, concat_axis=0, tiled=True
    )
    routed_sum = jnp.dot(
        weight_pick,
        returned.reshape(-1, model_width).astype(jnp.float32),
        precision=lax.Precision.HIGHEST,
        preferred_element_type=jnp.float32,
    )
    return (mixed_float + routed_sum).astype(jnp.bfloat16)

TOKEN_AXES = ("gx", "gyo", "core")


def solution(mesh):
    rows = P(TOKEN_AXES, None)
    split_mesh = jax.sharding.Mesh(
        mesh.devices.reshape(mesh.shape["gx"], mesh.shape["gy"] // 2, 2), TOKEN_AXES
    )
    in_specs = (
        rows,
        rows,
        P("gx", None),
        rows,
        rows,
        rows,
        P(),
        P(),
        P(),
        P(),
        P(("gyo", "core"), None),
        P(),
        rows,
        rows,
        P(TOKEN_AXES, None, None),
        P(TOKEN_AXES, None, None),
        P(TOKEN_AXES, None, None),
    )
    out_specs = rows
    return jax.shard_map(
        on_device, mesh=split_mesh, in_specs=in_specs, out_specs=out_specs, check_vma=False
    )
```

```python
import jax
import jax.numpy as jnp
from jax import lax
from jax.sharding import PartitionSpec as P
from jax.experimental import pallas as pl
from jax.experimental.pallas import tpu as pltpu

HEADS = 32
KV_HEADS = 4
HEAD_DIM = 128
ROOTS = 4
MIDS = 8


EPSILON = 1e-06


def node_bounds(node_owner, node_len, span_rows):
    labels = jnp.arange(node_owner.shape[0], dtype=jnp.int32)
    earlier = (node_owner[:, None] == node_owner[None, :]) & (labels[None, :] < labels[:, None])
    before = jnp.sum(jnp.where(earlier, node_len[None, :], 0), axis=1)
    starts = node_owner * span_rows + before
    return (starts, starts + node_len)


def key_labels(first_row, row_count, starts, finish):
    cache_rows = first_row + jnp.arange(row_count, dtype=jnp.int32)
    inside = (cache_rows[:, None] >= starts[None, :]) & (cache_rows[:, None] < finish[None, :])
    labels = jnp.arange(starts.shape[0], dtype=jnp.int32)
    return jnp.sum(jnp.where(inside, labels[None, :], 0), axis=1)


def path_nodes(requests, leaf_table, mid_parent, leaf_parent):
    picked = requests[:, None] == jnp.arange(leaf_table.shape[0], dtype=jnp.int32)[None, :]
    leaf_node = jnp.sum(jnp.where(picked, leaf_table[None, :], 0), axis=1)
    leaf_pick = leaf_node[:, None] == jnp.arange(leaf_parent.shape[0], dtype=jnp.int32)[None, :]
    middle_node = jnp.sum(jnp.where(leaf_pick, leaf_parent[None, :], 0), axis=1)
    middle_pick = middle_node[:, None] == jnp.arange(mid_parent.shape[0], dtype=jnp.int32)[None, :]
    root_node = jnp.sum(jnp.where(middle_pick, mid_parent[None, :], 0), axis=1)
    return jnp.stack([root_node, ROOTS + middle_node, ROOTS + MIDS + leaf_node], axis=1)


def masked_scores(query_heads, key_rows, allowed, head_scale):
    scores = (
        jnp.einsum("tgsd,kgd->gstk", query_heads, key_rows, preferred_element_type=jnp.float32)
        * head_scale
    )
    return jnp.where(allowed[None, None], scores, -jnp.inf)


def attention_kernel(q_ref, kc_ref, vc_ref, kn_ref, vn_ref, bf_ref, bn_ref, o_ref):
    head_scale = HEAD_DIM ** (-0.5)
    contract = (((1,), (1,)), ((), ()))
    far_keys = kc_ref[...]
    far_values = vc_ref[...]
    near_keys = kn_ref[...]
    near_values = vn_ref[...]
    far_bias = bf_ref[...]
    near_bias = bn_ref[...]
    for head in range(HEADS // KV_HEADS):
        cols = slice(head * HEAD_DIM, (head + 1) * HEAD_DIM)
        query = q_ref[:, cols]
        far = lax.dot_general(query, far_keys, contract, preferred_element_type=jnp.float32) + far_bias
        near = lax.dot_general(query, near_keys, contract, preferred_element_type=jnp.float32) + near_bias
        top = jnp.maximum(jnp.max(far, axis=1, keepdims=True), jnp.max(near, axis=1, keepdims=True))
        far_p = jnp.exp((far - top) * head_scale)
        near_p = jnp.exp((near - top) * head_scale)
        total = jnp.sum(far_p, axis=1, keepdims=True) + jnp.sum(near_p, axis=1, keepdims=True)
        summed = jnp.dot(
            far_p.astype(jnp.bfloat16), far_values, preferred_element_type=jnp.float32
        ) + jnp.dot(near_p.astype(jnp.bfloat16), near_values, preferred_element_type=jnp.float32)
        o_ref[:, cols] = (summed / total).astype(o_ref.dtype)


def tree_attention(queries, cache, new_kv, far_bias, near_bias):
    tokens = queries.shape[0]
    rows = cache.shape[0]
    group_cols = (HEADS // KV_HEADS) * HEAD_DIM
    return pl.pallas_call(
        attention_kernel,
        grid=(KV_HEADS,),
        in_specs=[
            pl.BlockSpec((tokens, group_cols), lambda g: (0, g)),
            pl.BlockSpec((rows, HEAD_DIM), lambda g: (0, g)),
            pl.BlockSpec((rows, HEAD_DIM), lambda g: (0, KV_HEADS + g)),
            pl.BlockSpec((tokens, HEAD_DIM), lambda g: (0, g)),
            pl.BlockSpec((tokens, HEAD_DIM), lambda g: (0, KV_HEADS + g)),
            pl.BlockSpec((tokens, rows), lambda g: (0, 0)),
            pl.BlockSpec((tokens, tokens), lambda g: (0, 0)),
        ],
        out_specs=pl.BlockSpec((tokens, group_cols), lambda g: (0, g)),
        out_shape=jax.ShapeDtypeStruct((tokens, HEADS * HEAD_DIM), jnp.bfloat16),
        compiler_params=pltpu.CompilerParams(vmem_limit_bytes=48 * 1024 * 1024),
    )(queries, cache, cache, new_kv, new_kv, far_bias, near_bias)


def on_device(
    queries,
    new_kv,
    kv_cache,
    residual,
    token_request,
    request_leaf,
    mid_parent,
    leaf_parent,
    node_owner,
    node_len,
    out_weight,
    norm_gain,
    route_experts,
    route_weights,
    expert_gate,
    expert_up,
    expert_down,
):
    tokens_here = queries.shape[0]
    model_width = residual.shape[1]
    group_size = HEADS // KV_HEADS
    kv_width = KV_HEADS * HEAD_DIM
    head_scale = HEAD_DIM ** (-0.5)
    requests = token_request[0]
    ancestry = path_nodes(requests, request_leaf[0], mid_parent, leaf_parent)
    span_rows = kv_cache.shape[0]
    starts, finish = node_bounds(node_owner, node_len, span_rows)
    positions = jnp.arange(tokens_here, dtype=jnp.int32)
    own_mask = (requests[:, None] == requests[None, :]) & (positions[None, :] <= positions[:, None])
    owners = lax.axis_size("gx")
    here = lax.axis_index("gx")
    pieces = [kv_cache] + [
        lax.ppermute(kv_cache, "gx", [(i, (i + shift) % owners) for i in range(owners)])
        for shift in range(1, owners)
    ]
    cache_all = jnp.concatenate(pieces, axis=0)
    owner_of = (here - jnp.arange(owners, dtype=jnp.int32)) % owners
    cache_rows = (owner_of[:, None] * span_rows + jnp.arange(span_rows, dtype=jnp.int32)[None, :]).reshape(-1)
    inside = (cache_rows[:, None] >= starts[None, :]) & (cache_rows[:, None] < finish[None, :])
    labels = jnp.sum(jnp.where(inside, jnp.arange(starts.shape[0], dtype=jnp.int32)[None, :], 0), axis=1)
    seen_mask = jnp.any(labels[None, :, None] == ancestry[:, None, :], axis=2)
    far_bias = jnp.where(seen_mask, 0.0, -jnp.inf).astype(jnp.float32)
    near_bias = jnp.where(own_mask, 0.0, -jnp.inf).astype(jnp.float32)
    attended = tree_attention(queries, cache_all, new_kv, far_bias, near_bias)
    shard_rows = out_weight.shape[0]
    shard_piece = lax.all_gather(out_weight, "gy", axis=0, tiled=True)
    block_count = shard_piece.shape[0] // shard_rows
    columns = attended.reshape(tokens_here, block_count, shard_rows)
    partial_value = jnp.einsum(
        "tnr,nrd->ntd",
        columns,
        shard_piece.reshape(block_count, shard_rows, model_width),
        preferred_element_type=jnp.float32,
    )
    partial_value = lax.optimization_barrier(partial_value.astype(jnp.bfloat16))
    projected = jnp.sum(partial_value.astype(jnp.float32), axis=0)
    mixed_state = (residual.astype(jnp.float32) + projected).astype(jnp.bfloat16)
    mixed_float = lax.optimization_barrier(mixed_state).astype(jnp.float32)
    normed = (
        mixed_float
        * lax.rsqrt(jnp.mean(mixed_float * mixed_float, axis=1, keepdims=True) + EPSILON)
        * norm_gain
    ).astype(jnp.bfloat16)
    top_count = route_experts.shape[1]
    expert_count = lax.axis_size("gx") * lax.axis_size("gy") * expert_gate.shape[0]
    capacity = max(2, (3 * tokens_here * top_count + 2 * expert_count - 1) // (2 * expert_count))
    slots = -(-capacity // 16) * 16
    flat_experts = route_experts.reshape(-1)
    onehot = (flat_experts[:, None] == jnp.arange(expert_count, dtype=jnp.int32)[None, :]).astype(
        jnp.int32
    )
    slot_ids = jnp.sum((jnp.cumsum(onehot, axis=0) - onehot) * onehot, axis=1)
    target = (flat_experts * slots + slot_ids).reshape(tokens_here, top_count)
    row_range = jnp.arange(expert_count * slots, dtype=jnp.int32)
    pick = jnp.any(target[None, :, :] == row_range[:, None, None], axis=2).astype(jnp.bfloat16)
    weight_pick = jnp.sum(
        jnp.where(target[:, None, :] == row_range[None, :, None], route_weights[:, None, :], 0.0),
        axis=2,
    )
    outgoing = jnp.dot(pick, normed, preferred_element_type=jnp.float32).astype(jnp.bfloat16)
    outgoing = outgoing.reshape(expert_count, slots, model_width)
    arrived = lax.all_to_all(outgoing, ("gx", "gy"), split_axis=0, concat_axis=0, tiled=True)
    stacked = arrived.reshape(-1, model_width)
    gate_act = jnp.dot(stacked, expert_gate[0], preferred_element_type=jnp.float32)
    up_act = jnp.dot(stacked, expert_up[0], preferred_element_type=jnp.float32)
    hidden = (jax.nn.silu(gate_act) * up_act).astype(jnp.bfloat16)
    expert_out = jnp.dot(hidden, expert_down[0], preferred_element_type=jnp.float32).astype(
        jnp.bfloat16
    )
    returned = lax.all_to_all(
        expert_out.reshape(arrived.shape), ("gx", "gy"), split_axis=0, concat_axis=0, tiled=True
    )
    routed_sum = jnp.dot(
        weight_pick,
        returned.reshape(-1, model_width).astype(jnp.float32),
        precision=lax.Precision.HIGHEST,
        preferred_element_type=jnp.float32,
    )
    return (mixed_float + routed_sum).astype(jnp.bfloat16)


def solution(mesh):
    in_specs = (
        P(("gx", "gy"), None),
        P(("gx", "gy"), None),
        P("gx", None),
        P(("gx", "gy"), None),
        P(("gx", "gy"), None),
        P(("gx", "gy"), None),
        P(),
        P(),
        P(),
        P(),
        P("gy", None),
        P(),
        P(("gx", "gy"), None),
        P(("gx", "gy"), None),
        P(("gx", "gy"), None, None),
        P(("gx", "gy"), None, None),
        P(("gx", "gy"), None, None),
    )
    out_specs = P(("gx", "gy"), None)
    return jax.shard_map(
        on_device, mesh=mesh, in_specs=in_specs, out_specs=out_specs, check_vma=False
    )
```

```python
import jax
import jax.numpy as jnp
from jax import lax
from jax.sharding import PartitionSpec as P
from jax.experimental import pallas as pl
from jax.experimental.pallas import tpu as pltpu

HEADS = 32
KV_HEADS = 4
HEAD_DIM = 128
ROOTS = 4
MIDS = 8


EPSILON = 1e-06


def node_bounds(node_owner, node_len, span_rows):
    labels = jnp.arange(node_owner.shape[0], dtype=jnp.int32)
    earlier = (node_owner[:, None] == node_owner[None, :]) & (labels[None, :] < labels[:, None])
    before = jnp.sum(jnp.where(earlier, node_len[None, :], 0), axis=1)
    starts = node_owner * span_rows + before
    return (starts, starts + node_len)


def key_labels(first_row, row_count, starts, finish):
    cache_rows = first_row + jnp.arange(row_count, dtype=jnp.int32)
    inside = (cache_rows[:, None] >= starts[None, :]) & (cache_rows[:, None] < finish[None, :])
    labels = jnp.arange(starts.shape[0], dtype=jnp.int32)
    return jnp.sum(jnp.where(inside, labels[None, :], 0), axis=1)


def path_nodes(requests, leaf_table, mid_parent, leaf_parent):
    picked = requests[:, None] == jnp.arange(leaf_table.shape[0], dtype=jnp.int32)[None, :]
    leaf_node = jnp.sum(jnp.where(picked, leaf_table[None, :], 0), axis=1)
    leaf_pick = leaf_node[:, None] == jnp.arange(leaf_parent.shape[0], dtype=jnp.int32)[None, :]
    middle_node = jnp.sum(jnp.where(leaf_pick, leaf_parent[None, :], 0), axis=1)
    middle_pick = middle_node[:, None] == jnp.arange(mid_parent.shape[0], dtype=jnp.int32)[None, :]
    root_node = jnp.sum(jnp.where(middle_pick, mid_parent[None, :], 0), axis=1)
    return jnp.stack([root_node, ROOTS + middle_node, ROOTS + MIDS + leaf_node], axis=1)


def masked_scores(query_heads, key_rows, allowed, head_scale):
    scores = (
        jnp.einsum("tgsd,kgd->gstk", query_heads, key_rows, preferred_element_type=jnp.float32)
        * head_scale
    )
    return jnp.where(allowed[None, None], scores, -jnp.inf)


def attention_kernel(q_ref, kc_ref, vc_ref, kn_ref, vn_ref, bf_ref, bn_ref, o_ref):
    head_scale = HEAD_DIM ** (-0.5)
    contract = (((1,), (1,)), ((), ()))
    far_keys = kc_ref[...]
    far_values = vc_ref[...]
    near_keys = kn_ref[...]
    near_values = vn_ref[...]
    far_bias = bf_ref[...]
    near_bias = bn_ref[...]
    for head in range(HEADS // KV_HEADS):
        cols = slice(head * HEAD_DIM, (head + 1) * HEAD_DIM)
        query = q_ref[:, cols]
        far = lax.dot_general(query, far_keys, contract, preferred_element_type=jnp.float32) + far_bias
        near = lax.dot_general(query, near_keys, contract, preferred_element_type=jnp.float32) + near_bias
        top = jnp.maximum(jnp.max(far, axis=1, keepdims=True), jnp.max(near, axis=1, keepdims=True))
        far_p = jnp.exp((far - top) * head_scale)
        near_p = jnp.exp((near - top) * head_scale)
        total = jnp.sum(far_p, axis=1, keepdims=True) + jnp.sum(near_p, axis=1, keepdims=True)
        summed = jnp.dot(
            far_p.astype(jnp.bfloat16), far_values, preferred_element_type=jnp.float32
        ) + jnp.dot(near_p.astype(jnp.bfloat16), near_values, preferred_element_type=jnp.float32)
        o_ref[:, cols] = (summed / total).astype(o_ref.dtype)


def tree_attention(queries, cache, new_kv, far_bias, near_bias):
    tokens = queries.shape[0]
    rows = cache.shape[0]
    group_cols = (HEADS // KV_HEADS) * HEAD_DIM
    return pl.pallas_call(
        attention_kernel,
        grid=(KV_HEADS,),
        in_specs=[
            pl.BlockSpec((tokens, group_cols), lambda g: (0, g)),
            pl.BlockSpec((rows, HEAD_DIM), lambda g: (0, g)),
            pl.BlockSpec((rows, HEAD_DIM), lambda g: (0, KV_HEADS + g)),
            pl.BlockSpec((tokens, HEAD_DIM), lambda g: (0, g)),
            pl.BlockSpec((tokens, HEAD_DIM), lambda g: (0, KV_HEADS + g)),
            pl.BlockSpec((tokens, rows), lambda g: (0, 0)),
            pl.BlockSpec((tokens, tokens), lambda g: (0, 0)),
        ],
        out_specs=pl.BlockSpec((tokens, group_cols), lambda g: (0, g)),
        out_shape=jax.ShapeDtypeStruct((tokens, HEADS * HEAD_DIM), jnp.bfloat16),
        compiler_params=pltpu.CompilerParams(vmem_limit_bytes=48 * 1024 * 1024),
    )(queries, cache, cache, new_kv, new_kv, far_bias, near_bias)


def on_device(
    queries,
    new_kv,
    kv_cache,
    residual,
    token_request,
    request_leaf,
    mid_parent,
    leaf_parent,
    node_owner,
    node_len,
    out_weight,
    norm_gain,
    route_experts,
    route_weights,
    expert_gate,
    expert_up,
    expert_down,
):
    tokens_here = queries.shape[0]
    model_width = residual.shape[1]
    group_size = HEADS // KV_HEADS
    kv_width = KV_HEADS * HEAD_DIM
    head_scale = HEAD_DIM ** (-0.5)
    requests = token_request[0]
    ancestry = path_nodes(requests, request_leaf[0], mid_parent, leaf_parent)
    span_rows = kv_cache.shape[0]
    starts, finish = node_bounds(node_owner, node_len, span_rows)
    positions = jnp.arange(tokens_here, dtype=jnp.int32)
    own_mask = (requests[:, None] == requests[None, :]) & (positions[None, :] <= positions[:, None])
    cache_all = lax.all_gather(kv_cache, "gx", axis=0, tiled=True)
    labels = key_labels(0, cache_all.shape[0], starts, finish)
    seen_mask = jnp.any(labels[None, :, None] == ancestry[:, None, :], axis=2)
    far_bias = jnp.where(seen_mask, 0.0, -jnp.inf).astype(jnp.float32)
    near_bias = jnp.where(own_mask, 0.0, -jnp.inf).astype(jnp.float32)
    attended = tree_attention(queries, cache_all, new_kv, far_bias, near_bias)
    shard_rows = out_weight.shape[0]
    core = lax.axis_index("core")
    swap = [(0, 1), (1, 0)]
    row_owners = lax.axis_size("gyo")
    row_here = lax.axis_index("gyo")
    parity_rows = jnp.stack(
        [out_weight]
        + [
            lax.ppermute(out_weight, "gyo", [(i, (i + shift) % row_owners) for i in range(row_owners)])
            for shift in range(1, row_owners)
        ],
        axis=0,
    )
    group_of = (row_here - jnp.arange(row_owners, dtype=jnp.int32)) % row_owners
    partner = lax.ppermute(attended, "core", swap)
    pair = jnp.concatenate([attended, partner], axis=0)
    columns = jnp.stack(
        [
            lax.dynamic_slice_in_dim(pair, (2 * group_of[group] + core) * shard_rows, shard_rows, axis=1)
            for group in range(parity_rows.shape[0])
        ],
        axis=1,
    )
    partial_value = jnp.einsum(
        "tnr,nrd->ntd", columns, parity_rows, preferred_element_type=jnp.float32
    )
    partial_value = lax.optimization_barrier(partial_value.astype(jnp.bfloat16))
    pair_sum = jnp.sum(partial_value.astype(jnp.float32), axis=0)
    projected = pair_sum[:tokens_here] + lax.ppermute(pair_sum[tokens_here:], "core", swap)
    mixed_state = (residual.astype(jnp.float32) + projected).astype(jnp.bfloat16)
    mixed_float = lax.optimization_barrier(mixed_state).astype(jnp.float32)
    normed = (
        mixed_float
        * lax.rsqrt(jnp.mean(mixed_float * mixed_float, axis=1, keepdims=True) + EPSILON)
        * norm_gain
    ).astype(jnp.bfloat16)
    top_count = route_experts.shape[1]
    expert_count = lax.axis_size("gx") * lax.axis_size("gyo") * lax.axis_size("core") * expert_gate.shape[0]
    capacity = max(2, (3 * tokens_here * top_count + 2 * expert_count - 1) // (2 * expert_count))
    slots = -(-capacity // 16) * 16
    flat_experts = route_experts.reshape(-1)
    onehot = (flat_experts[:, None] == jnp.arange(expert_count, dtype=jnp.int32)[None, :]).astype(
        jnp.int32
    )
    slot_ids = jnp.sum((jnp.cumsum(onehot, axis=0) - onehot) * onehot, axis=1)
    target = (flat_experts * slots + slot_ids).reshape(tokens_here, top_count)
    row_range = jnp.arange(expert_count * slots, dtype=jnp.int32)
    pick = jnp.any(target[None, :, :] == row_range[:, None, None], axis=2).astype(jnp.bfloat16)
    weight_pick = jnp.sum(
        jnp.where(target[:, None, :] == row_range[None, :, None], route_weights[:, None, :], 0.0),
        axis=2,
    )
    outgoing = jnp.dot(pick, normed, preferred_element_type=jnp.float32).astype(jnp.bfloat16)
    outgoing = outgoing.reshape(expert_count, slots, model_width)
    arrived = lax.all_to_all(outgoing, TOKEN_AXES, split_axis=0, concat_axis=0, tiled=True)
    stacked = arrived.reshape(-1, model_width)
    gate_act = jnp.dot(stacked, expert_gate[0], preferred_element_type=jnp.float32)
    up_act = jnp.dot(stacked, expert_up[0], preferred_element_type=jnp.float32)
    hidden = (jax.nn.silu(gate_act) * up_act).astype(jnp.bfloat16)
    expert_out = jnp.dot(hidden, expert_down[0], preferred_element_type=jnp.float32).astype(
        jnp.bfloat16
    )
    returned = lax.all_to_all(
        expert_out.reshape(arrived.shape), TOKEN_AXES, split_axis=0, concat_axis=0, tiled=True
    )
    routed_sum = jnp.dot(
        weight_pick,
        returned.reshape(-1, model_width).astype(jnp.float32),
        precision=lax.Precision.HIGHEST,
        preferred_element_type=jnp.float32,
    )
    return (mixed_float + routed_sum).astype(jnp.bfloat16)

TOKEN_AXES = ("gx", "gyo", "core")


def solution(mesh):
    rows = P(TOKEN_AXES, None)
    split_mesh = jax.sharding.Mesh(
        mesh.devices.reshape(mesh.shape["gx"], mesh.shape["gy"] // 2, 2), TOKEN_AXES
    )
    in_specs = (
        rows,
        rows,
        P("gx", None),
        rows,
        rows,
        rows,
        P(),
        P(),
        P(),
        P(),
        P(("gyo", "core"), None),
        P(),
        rows,
        rows,
        P(TOKEN_AXES, None, None),
        P(TOKEN_AXES, None, None),
        P(TOKEN_AXES, None, None),
    )
    out_specs = rows
    return jax.shard_map(
        on_device, mesh=split_mesh, in_specs=in_specs, out_specs=out_specs, check_vma=False
    )
```

```python
import jax
import jax.numpy as jnp
from jax import lax
from jax.sharding import PartitionSpec as P
from jax.experimental import pallas as pl
from jax.experimental.pallas import tpu as pltpu

HEADS = 32
KV_HEADS = 4
HEAD_DIM = 128
ROOTS = 4
MIDS = 8


EPSILON = 1e-06


def node_bounds(node_owner, node_len, span_rows):
    labels = jnp.arange(node_owner.shape[0], dtype=jnp.int32)
    earlier = (node_owner[:, None] == node_owner[None, :]) & (labels[None, :] < labels[:, None])
    before = jnp.sum(jnp.where(earlier, node_len[None, :], 0), axis=1)
    starts = node_owner * span_rows + before
    return (starts, starts + node_len)


def key_labels(first_row, row_count, starts, finish):
    cache_rows = first_row + jnp.arange(row_count, dtype=jnp.int32)
    inside = (cache_rows[:, None] >= starts[None, :]) & (cache_rows[:, None] < finish[None, :])
    labels = jnp.arange(starts.shape[0], dtype=jnp.int32)
    return jnp.sum(jnp.where(inside, labels[None, :], 0), axis=1)


def path_nodes(requests, leaf_table, mid_parent, leaf_parent):
    picked = requests[:, None] == jnp.arange(leaf_table.shape[0], dtype=jnp.int32)[None, :]
    leaf_node = jnp.sum(jnp.where(picked, leaf_table[None, :], 0), axis=1)
    leaf_pick = leaf_node[:, None] == jnp.arange(leaf_parent.shape[0], dtype=jnp.int32)[None, :]
    middle_node = jnp.sum(jnp.where(leaf_pick, leaf_parent[None, :], 0), axis=1)
    middle_pick = middle_node[:, None] == jnp.arange(mid_parent.shape[0], dtype=jnp.int32)[None, :]
    root_node = jnp.sum(jnp.where(middle_pick, mid_parent[None, :], 0), axis=1)
    return jnp.stack([root_node, ROOTS + middle_node, ROOTS + MIDS + leaf_node], axis=1)


def masked_scores(query_heads, key_rows, allowed, head_scale):
    scores = (
        jnp.einsum("tgsd,kgd->gstk", query_heads, key_rows, preferred_element_type=jnp.float32)
        * head_scale
    )
    return jnp.where(allowed[None, None], scores, -jnp.inf)


def attention_kernel(q_ref, kc_ref, vc_ref, kn_ref, vn_ref, bf_ref, bn_ref, o_ref):
    head_scale = HEAD_DIM ** (-0.5)
    contract = (((1,), (1,)), ((), ()))
    far_keys = kc_ref[...]
    far_values = vc_ref[...]
    near_keys = kn_ref[...]
    near_values = vn_ref[...]
    far_bias = bf_ref[...]
    near_bias = bn_ref[...]
    for head in range(HEADS // KV_HEADS):
        cols = slice(head * HEAD_DIM, (head + 1) * HEAD_DIM)
        query = q_ref[:, cols]
        far = lax.dot_general(query, far_keys, contract, preferred_element_type=jnp.float32) + far_bias
        near = lax.dot_general(query, near_keys, contract, preferred_element_type=jnp.float32) + near_bias
        top = jnp.maximum(jnp.max(far, axis=1, keepdims=True), jnp.max(near, axis=1, keepdims=True))
        far_p = jnp.exp((far - top) * head_scale)
        near_p = jnp.exp((near - top) * head_scale)
        total = jnp.sum(far_p, axis=1, keepdims=True) + jnp.sum(near_p, axis=1, keepdims=True)
        summed = jnp.dot(
            far_p.astype(jnp.bfloat16), far_values, preferred_element_type=jnp.float32
        ) + jnp.dot(near_p.astype(jnp.bfloat16), near_values, preferred_element_type=jnp.float32)
        o_ref[:, cols] = (summed / total).astype(o_ref.dtype)


def tree_attention(queries, cache, new_kv, far_bias, near_bias):
    tokens = queries.shape[0]
    rows = cache.shape[0]
    group_cols = (HEADS // KV_HEADS) * HEAD_DIM
    return pl.pallas_call(
        attention_kernel,
        grid=(KV_HEADS,),
        in_specs=[
            pl.BlockSpec((tokens, group_cols), lambda g: (0, g)),
            pl.BlockSpec((rows, HEAD_DIM), lambda g: (0, g)),
            pl.BlockSpec((rows, HEAD_DIM), lambda g: (0, KV_HEADS + g)),
            pl.BlockSpec((tokens, HEAD_DIM), lambda g: (0, g)),
            pl.BlockSpec((tokens, HEAD_DIM), lambda g: (0, KV_HEADS + g)),
            pl.BlockSpec((tokens, rows), lambda g: (0, 0)),
            pl.BlockSpec((tokens, tokens), lambda g: (0, 0)),
        ],
        out_specs=pl.BlockSpec((tokens, group_cols), lambda g: (0, g)),
        out_shape=jax.ShapeDtypeStruct((tokens, HEADS * HEAD_DIM), jnp.bfloat16),
        compiler_params=pltpu.CompilerParams(vmem_limit_bytes=48 * 1024 * 1024),
    )(queries, cache, cache, new_kv, new_kv, far_bias, near_bias)


def projection_kernel(a_ref, w_ref, o_ref):
    @pl.when(pl.program_id(0) == 0)
    def _():
        o_ref[...] = jnp.zeros_like(o_ref)

    part = jnp.dot(a_ref[...], w_ref[...], preferred_element_type=jnp.float32)
    o_ref[...] += part.astype(jnp.bfloat16).astype(jnp.float32)


def projection(attended, weight, group_rows):
    tokens = attended.shape[0]
    width = weight.shape[1]
    return pl.pallas_call(
        projection_kernel,
        grid=(weight.shape[0] // group_rows,),
        in_specs=[
            pl.BlockSpec((tokens, group_rows), lambda j: (0, j)),
            pl.BlockSpec((group_rows, width), lambda j: (j, 0)),
        ],
        out_specs=pl.BlockSpec((tokens, width), lambda j: (0, 0)),
        out_shape=jax.ShapeDtypeStruct((tokens, width), jnp.float32),
    )(attended, weight)


def on_device(
    queries,
    new_kv,
    kv_cache,
    residual,
    token_request,
    request_leaf,
    mid_parent,
    leaf_parent,
    node_owner,
    node_len,
    out_weight,
    norm_gain,
    route_experts,
    route_weights,
    expert_gate,
    expert_up,
    expert_down,
):
    tokens_here = queries.shape[0]
    model_width = residual.shape[1]
    group_size = HEADS // KV_HEADS
    kv_width = KV_HEADS * HEAD_DIM
    head_scale = HEAD_DIM ** (-0.5)
    requests = token_request[0]
    ancestry = path_nodes(requests, request_leaf[0], mid_parent, leaf_parent)
    span_rows = kv_cache.shape[0]
    starts, finish = node_bounds(node_owner, node_len, span_rows)
    positions = jnp.arange(tokens_here, dtype=jnp.int32)
    own_mask = (requests[:, None] == requests[None, :]) & (positions[None, :] <= positions[:, None])
    cache_all = lax.all_gather(kv_cache, "gx", axis=0, tiled=True)
    labels = key_labels(0, cache_all.shape[0], starts, finish)
    seen_mask = jnp.any(labels[None, :, None] == ancestry[:, None, :], axis=2)
    far_bias = jnp.where(seen_mask, 0.0, -jnp.inf).astype(jnp.float32)
    near_bias = jnp.where(own_mask, 0.0, -jnp.inf).astype(jnp.float32)
    attended = tree_attention(queries, cache_all, new_kv, far_bias, near_bias)
    shard_rows = out_weight.shape[0]
    shard_piece = lax.all_gather(out_weight, "gy", axis=0, tiled=True)
    projected = projection(attended, shard_piece, shard_rows)
    mixed_state = (residual.astype(jnp.float32) + projected).astype(jnp.bfloat16)
    mixed_float = lax.optimization_barrier(mixed_state).astype(jnp.float32)
    normed = (
        mixed_float
        * lax.rsqrt(jnp.mean(mixed_float * mixed_float, axis=1, keepdims=True) + EPSILON)
        * norm_gain
    ).astype(jnp.bfloat16)
    top_count = route_experts.shape[1]
    expert_count = lax.axis_size("gx") * lax.axis_size("gy") * expert_gate.shape[0]
    capacity = max(2, (3 * tokens_here * top_count + 2 * expert_count - 1) // (2 * expert_count))
    slots = -(-capacity // 16) * 16
    flat_experts = route_experts.reshape(-1)
    onehot = (flat_experts[:, None] == jnp.arange(expert_count, dtype=jnp.int32)[None, :]).astype(
        jnp.int32
    )
    slot_ids = jnp.sum((jnp.cumsum(onehot, axis=0) - onehot) * onehot, axis=1)
    target = (flat_experts * slots + slot_ids).reshape(tokens_here, top_count)
    row_range = jnp.arange(expert_count * slots, dtype=jnp.int32)
    pick = jnp.any(target[None, :, :] == row_range[:, None, None], axis=2).astype(jnp.bfloat16)
    weight_pick = jnp.sum(
        jnp.where(target[:, None, :] == row_range[None, :, None], route_weights[:, None, :], 0.0),
        axis=2,
    )
    outgoing = jnp.dot(pick, normed, preferred_element_type=jnp.float32).astype(jnp.bfloat16)
    outgoing = outgoing.reshape(expert_count, slots, model_width)
    arrived = lax.all_to_all(outgoing, ("gx", "gy"), split_axis=0, concat_axis=0, tiled=True)
    stacked = arrived.reshape(-1, model_width)
    gate_act = jnp.dot(stacked, expert_gate[0], preferred_element_type=jnp.float32)
    up_act = jnp.dot(stacked, expert_up[0], preferred_element_type=jnp.float32)
    hidden = (jax.nn.silu(gate_act) * up_act).astype(jnp.bfloat16)
    expert_out = jnp.dot(hidden, expert_down[0], preferred_element_type=jnp.float32).astype(
        jnp.bfloat16
    )
    returned = lax.all_to_all(
        expert_out.reshape(arrived.shape), ("gx", "gy"), split_axis=0, concat_axis=0, tiled=True
    )
    routed_sum = jnp.dot(
        weight_pick,
        returned.reshape(-1, model_width).astype(jnp.float32),
        precision=lax.Precision.HIGH,
        preferred_element_type=jnp.float32,
    )
    return (mixed_float + routed_sum).astype(jnp.bfloat16)

def solution(mesh):
    in_specs = (
        P(("gx", "gy"), None),
        P(("gx", "gy"), None),
        P("gx", None),
        P(("gx", "gy"), None),
        P(("gx", "gy"), None),
        P(("gx", "gy"), None),
        P(),
        P(),
        P(),
        P(),
        P("gy", None),
        P(),
        P(("gx", "gy"), None),
        P(("gx", "gy"), None),
        P(("gx", "gy"), None, None),
        P(("gx", "gy"), None, None),
        P(("gx", "gy"), None, None),
    )
    out_specs = P(("gx", "gy"), None)
    return jax.shard_map(
        on_device, mesh=mesh, in_specs=in_specs, out_specs=out_specs, check_vma=False
    )
```

```python
import jax
import jax.numpy as jnp
from jax import lax
from jax.sharding import PartitionSpec as P
from jax.experimental import pallas as pl
from jax.experimental.pallas import tpu as pltpu

HEADS = 32
KV_HEADS = 4
HEAD_DIM = 128
ROOTS = 4
MIDS = 8


EPSILON = 1e-06


def node_bounds(node_owner, node_len, span_rows):
    labels = jnp.arange(node_owner.shape[0], dtype=jnp.int32)
    earlier = (node_owner[:, None] == node_owner[None, :]) & (labels[None, :] < labels[:, None])
    before = jnp.sum(jnp.where(earlier, node_len[None, :], 0), axis=1)
    starts = node_owner * span_rows + before
    return (starts, starts + node_len)


def key_labels(first_row, row_count, starts, finish):
    cache_rows = first_row + jnp.arange(row_count, dtype=jnp.int32)
    inside = (cache_rows[:, None] >= starts[None, :]) & (cache_rows[:, None] < finish[None, :])
    labels = jnp.arange(starts.shape[0], dtype=jnp.int32)
    return jnp.sum(jnp.where(inside, labels[None, :], 0), axis=1)


def path_nodes(requests, leaf_table, mid_parent, leaf_parent):
    picked = requests[:, None] == jnp.arange(leaf_table.shape[0], dtype=jnp.int32)[None, :]
    leaf_node = jnp.sum(jnp.where(picked, leaf_table[None, :], 0), axis=1)
    leaf_pick = leaf_node[:, None] == jnp.arange(leaf_parent.shape[0], dtype=jnp.int32)[None, :]
    middle_node = jnp.sum(jnp.where(leaf_pick, leaf_parent[None, :], 0), axis=1)
    middle_pick = middle_node[:, None] == jnp.arange(mid_parent.shape[0], dtype=jnp.int32)[None, :]
    root_node = jnp.sum(jnp.where(middle_pick, mid_parent[None, :], 0), axis=1)
    return jnp.stack([root_node, ROOTS + middle_node, ROOTS + MIDS + leaf_node], axis=1)


def masked_scores(query_heads, key_rows, allowed, head_scale):
    scores = (
        jnp.einsum("tgsd,kgd->gstk", query_heads, key_rows, preferred_element_type=jnp.float32)
        * head_scale
    )
    return jnp.where(allowed[None, None], scores, -jnp.inf)


def attention_kernel(q_ref, kc_ref, vc_ref, kn_ref, vn_ref, bf_ref, bn_ref, o_ref):
    head_scale = HEAD_DIM ** (-0.5)
    contract = (((1,), (1,)), ((), ()))
    far_keys = kc_ref[...]
    far_values = vc_ref[...]
    near_keys = kn_ref[...]
    near_values = vn_ref[...]
    far_bias = bf_ref[...]
    near_bias = bn_ref[...]
    for head in range(HEADS // KV_HEADS):
        cols = slice(head * HEAD_DIM, (head + 1) * HEAD_DIM)
        query = q_ref[:, cols]
        far = lax.dot_general(query, far_keys, contract, preferred_element_type=jnp.float32) + far_bias
        near = lax.dot_general(query, near_keys, contract, preferred_element_type=jnp.float32) + near_bias
        top = jnp.maximum(jnp.max(far, axis=1, keepdims=True), jnp.max(near, axis=1, keepdims=True))
        far_p = jnp.exp((far - top) * head_scale)
        near_p = jnp.exp((near - top) * head_scale)
        total = jnp.sum(far_p, axis=1, keepdims=True) + jnp.sum(near_p, axis=1, keepdims=True)
        summed = jnp.dot(
            far_p.astype(jnp.bfloat16), far_values, preferred_element_type=jnp.float32
        ) + jnp.dot(near_p.astype(jnp.bfloat16), near_values, preferred_element_type=jnp.float32)
        o_ref[:, cols] = (summed / total).astype(o_ref.dtype)


def tree_attention(queries, cache, new_kv, far_bias, near_bias):
    tokens = queries.shape[0]
    rows = cache.shape[0]
    group_cols = (HEADS // KV_HEADS) * HEAD_DIM
    local_heads = cache.shape[1] // (2 * HEAD_DIM)
    return pl.pallas_call(
        attention_kernel,
        grid=(local_heads,),
        in_specs=[
            pl.BlockSpec((tokens, group_cols), lambda g: (0, g)),
            pl.BlockSpec((rows, HEAD_DIM), lambda g: (0, g)),
            pl.BlockSpec((rows, HEAD_DIM), lambda g: (0, local_heads + g)),
            pl.BlockSpec((tokens, HEAD_DIM), lambda g: (0, g)),
            pl.BlockSpec((tokens, HEAD_DIM), lambda g: (0, local_heads + g)),
            pl.BlockSpec((tokens, rows), lambda g: (0, 0)),
            pl.BlockSpec((tokens, tokens), lambda g: (0, 0)),
        ],
        out_specs=pl.BlockSpec((tokens, group_cols), lambda g: (0, g)),
        out_shape=jax.ShapeDtypeStruct((tokens, local_heads * group_cols), jnp.bfloat16),
        compiler_params=pltpu.CompilerParams(vmem_limit_bytes=48 * 1024 * 1024),
    )(queries, cache, cache, new_kv, new_kv, far_bias, near_bias)


def head_half(x, half, width):
    return lax.dynamic_slice_in_dim(x, half * width, width, axis=1)


def kv_half(x, half):
    kv_width = KV_HEADS * HEAD_DIM
    width = kv_width // 2
    return jnp.concatenate(
        [head_half(x[:, :kv_width], half, width), head_half(x[:, kv_width:], half, width)], axis=1
    )


def projection_kernel(a_ref, w_ref, o_ref):
    @pl.when(pl.program_id(0) == 0)
    def _():
        o_ref[...] = jnp.zeros_like(o_ref)

    part = jnp.dot(a_ref[...], w_ref[...], preferred_element_type=jnp.float32)
    o_ref[...] += part.astype(jnp.bfloat16).astype(jnp.float32)


def projection(attended, weight, group_rows):
    tokens = attended.shape[0]
    width = weight.shape[1]
    return pl.pallas_call(
        projection_kernel,
        grid=(weight.shape[0] // group_rows,),
        in_specs=[
            pl.BlockSpec((tokens, group_rows), lambda j: (0, j)),
            pl.BlockSpec((group_rows, width), lambda j: (j, 0)),
        ],
        out_specs=pl.BlockSpec((tokens, width), lambda j: (0, 0)),
        out_shape=jax.ShapeDtypeStruct((tokens, width), jnp.float32),
    )(attended, weight)


def on_device(
    queries,
    new_kv,
    kv_cache,
    residual,
    token_request,
    request_leaf,
    mid_parent,
    leaf_parent,
    node_owner,
    node_len,
    out_weight,
    norm_gain,
    route_experts,
    route_weights,
    expert_gate,
    expert_up,
    expert_down,
):
    tokens_here = queries.shape[0]
    model_width = residual.shape[1]
    group_size = HEADS // KV_HEADS
    kv_width = KV_HEADS * HEAD_DIM
    head_scale = HEAD_DIM ** (-0.5)
    requests = token_request[0]
    ancestry = path_nodes(requests, request_leaf[0], mid_parent, leaf_parent)
    span_rows = kv_cache.shape[0]
    starts, finish = node_bounds(node_owner, node_len, span_rows)
    positions = jnp.arange(tokens_here, dtype=jnp.int32)
    own_mask = (requests[:, None] == requests[None, :]) & (positions[None, :] <= positions[:, None])
    core = lax.axis_index("core")
    other_core = 1 - core
    swap = [(0, 1), (1, 0)]
    cache_mine = lax.all_gather(kv_half(kv_cache, core), "gx", axis=0, tiled=True)
    cache_other = lax.ppermute(cache_mine, "core", swap)
    labels = key_labels(0, cache_mine.shape[0], starts, finish)
    seen_mask = jnp.any(labels[None, :, None] == ancestry[:, None, :], axis=2)
    far_bias = jnp.where(seen_mask, 0.0, -jnp.inf).astype(jnp.float32)
    near_bias = jnp.where(own_mask, 0.0, -jnp.inf).astype(jnp.float32)
    query_cols = queries.shape[1] // 2
    attended_mine = tree_attention(
        head_half(queries, core, query_cols), cache_mine, kv_half(new_kv, core), far_bias, near_bias
    )
    attended_other = tree_attention(
        head_half(queries, other_core, query_cols), cache_other, kv_half(new_kv, other_core), far_bias, near_bias
    )
    attended = jnp.where(
        core == 0,
        jnp.concatenate([attended_mine, attended_other], axis=1),
        jnp.concatenate([attended_other, attended_mine], axis=1),
    )
    shard_rows = out_weight.shape[0]
    shard_piece = lax.all_gather(out_weight, ("gyo", "core"), axis=0, tiled=True)
    projected = projection(attended, shard_piece, shard_rows)
    mixed_state = (residual.astype(jnp.float32) + projected).astype(jnp.bfloat16)
    mixed_float = lax.optimization_barrier(mixed_state).astype(jnp.float32)
    normed = (
        mixed_float
        * lax.rsqrt(jnp.mean(mixed_float * mixed_float, axis=1, keepdims=True) + EPSILON)
        * norm_gain
    ).astype(jnp.bfloat16)
    top_count = route_experts.shape[1]
    expert_count = lax.axis_size("gx") * lax.axis_size("gyo") * lax.axis_size("core") * expert_gate.shape[0]
    capacity = max(2, (3 * tokens_here * top_count + 2 * expert_count - 1) // (2 * expert_count))
    slots = -(-capacity // 16) * 16
    flat_experts = route_experts.reshape(-1)
    onehot = (flat_experts[:, None] == jnp.arange(expert_count, dtype=jnp.int32)[None, :]).astype(
        jnp.int32
    )
    slot_ids = jnp.sum((jnp.cumsum(onehot, axis=0) - onehot) * onehot, axis=1)
    target = (flat_experts * slots + slot_ids).reshape(tokens_here, top_count)
    row_range = jnp.arange(expert_count * slots, dtype=jnp.int32)
    pick = jnp.any(target[None, :, :] == row_range[:, None, None], axis=2).astype(jnp.bfloat16)
    weight_pick = jnp.sum(
        jnp.where(target[:, None, :] == row_range[None, :, None], route_weights[:, None, :], 0.0),
        axis=2,
    )
    outgoing = jnp.dot(pick, normed, preferred_element_type=jnp.float32).astype(jnp.bfloat16)
    outgoing = outgoing.reshape(expert_count, slots, model_width)
    arrived = lax.all_to_all(outgoing, TOKEN_AXES, split_axis=0, concat_axis=0, tiled=True)
    stacked = arrived.reshape(-1, model_width)
    gate_act = jnp.dot(stacked, expert_gate[0], preferred_element_type=jnp.float32)
    up_act = jnp.dot(stacked, expert_up[0], preferred_element_type=jnp.float32)
    hidden = (jax.nn.silu(gate_act) * up_act).astype(jnp.bfloat16)
    expert_out = jnp.dot(hidden, expert_down[0], preferred_element_type=jnp.float32).astype(
        jnp.bfloat16
    )
    returned = lax.all_to_all(
        expert_out.reshape(arrived.shape), TOKEN_AXES, split_axis=0, concat_axis=0, tiled=True
    )
    routed_sum = jnp.dot(
        weight_pick,
        returned.reshape(-1, model_width).astype(jnp.float32),
        precision=lax.Precision.HIGH,
        preferred_element_type=jnp.float32,
    )
    return (mixed_float + routed_sum).astype(jnp.bfloat16)

TOKEN_AXES = ("gx", "gyo", "core")


def solution(mesh):
    rows = P(TOKEN_AXES, None)
    split_mesh = jax.sharding.Mesh(
        mesh.devices.reshape(mesh.shape["gx"], mesh.shape["gy"] // 2, 2), TOKEN_AXES
    )
    in_specs = (
        rows,
        rows,
        P("gx", None),
        rows,
        rows,
        rows,
        P(),
        P(),
        P(),
        P(),
        P(("gyo", "core"), None),
        P(),
        rows,
        rows,
        P(TOKEN_AXES, None, None),
        P(TOKEN_AXES, None, None),
        P(TOKEN_AXES, None, None),
    )
    out_specs = rows
    return jax.shard_map(
        on_device, mesh=split_mesh, in_specs=in_specs, out_specs=out_specs, check_vma=False
    )
```

```python
import jax
import jax.numpy as jnp
from jax import lax
from jax.sharding import PartitionSpec as P
from jax.experimental import pallas as pl
from jax.experimental.pallas import tpu as pltpu

HEADS = 32
KV_HEADS = 4
HEAD_DIM = 128
ROOTS = 4
MIDS = 8


EPSILON = 1e-06


def node_bounds(node_owner, node_len, span_rows):
    labels = jnp.arange(node_owner.shape[0], dtype=jnp.int32)
    earlier = (node_owner[:, None] == node_owner[None, :]) & (labels[None, :] < labels[:, None])
    before = jnp.sum(jnp.where(earlier, node_len[None, :], 0), axis=1)
    starts = node_owner * span_rows + before
    return (starts, starts + node_len)


def key_labels(first_row, row_count, starts, finish):
    cache_rows = first_row + jnp.arange(row_count, dtype=jnp.int32)
    inside = (cache_rows[:, None] >= starts[None, :]) & (cache_rows[:, None] < finish[None, :])
    labels = jnp.arange(starts.shape[0], dtype=jnp.int32)
    return jnp.sum(jnp.where(inside, labels[None, :], 0), axis=1)


def path_nodes(requests, leaf_table, mid_parent, leaf_parent):
    picked = requests[:, None] == jnp.arange(leaf_table.shape[0], dtype=jnp.int32)[None, :]
    leaf_node = jnp.sum(jnp.where(picked, leaf_table[None, :], 0), axis=1)
    leaf_pick = leaf_node[:, None] == jnp.arange(leaf_parent.shape[0], dtype=jnp.int32)[None, :]
    middle_node = jnp.sum(jnp.where(leaf_pick, leaf_parent[None, :], 0), axis=1)
    middle_pick = middle_node[:, None] == jnp.arange(mid_parent.shape[0], dtype=jnp.int32)[None, :]
    root_node = jnp.sum(jnp.where(middle_pick, mid_parent[None, :], 0), axis=1)
    return jnp.stack([root_node, ROOTS + middle_node, ROOTS + MIDS + leaf_node], axis=1)


def masked_scores(query_heads, key_rows, allowed, head_scale):
    scores = (
        jnp.einsum("tgsd,kgd->gstk", query_heads, key_rows, preferred_element_type=jnp.float32)
        * head_scale
    )
    return jnp.where(allowed[None, None], scores, -jnp.inf)


def attention_kernel(q_ref, kc_ref, vc_ref, kn_ref, vn_ref, bf_ref, bn_ref, o_ref):
    head_scale = HEAD_DIM ** (-0.5)
    contract = (((1,), (1,)), ((), ()))
    far_keys = kc_ref[...]
    far_values = vc_ref[...]
    near_keys = kn_ref[...]
    near_values = vn_ref[...]
    far_bias = bf_ref[...]
    near_bias = bn_ref[...]
    for head in range(HEADS // KV_HEADS):
        cols = slice(head * HEAD_DIM, (head + 1) * HEAD_DIM)
        query = q_ref[:, cols]
        far = lax.dot_general(query, far_keys, contract, preferred_element_type=jnp.float32) + far_bias
        near = lax.dot_general(query, near_keys, contract, preferred_element_type=jnp.float32) + near_bias
        top = jnp.maximum(jnp.max(far, axis=1, keepdims=True), jnp.max(near, axis=1, keepdims=True))
        far_p = jnp.exp((far - top) * head_scale)
        near_p = jnp.exp((near - top) * head_scale)
        total = jnp.sum(far_p, axis=1, keepdims=True) + jnp.sum(near_p, axis=1, keepdims=True)
        summed = jnp.dot(
            far_p.astype(jnp.bfloat16), far_values, preferred_element_type=jnp.float32
        ) + jnp.dot(near_p.astype(jnp.bfloat16), near_values, preferred_element_type=jnp.float32)
        o_ref[:, cols] = (summed / total).astype(o_ref.dtype)


def tree_attention(queries, cache, new_kv, far_bias, near_bias):
    tokens = queries.shape[0]
    rows = cache.shape[0]
    group_cols = (HEADS // KV_HEADS) * HEAD_DIM
    local_heads = cache.shape[1] // (2 * HEAD_DIM)
    return pl.pallas_call(
        attention_kernel,
        grid=(local_heads,),
        in_specs=[
            pl.BlockSpec((tokens, group_cols), lambda g: (0, g)),
            pl.BlockSpec((rows, HEAD_DIM), lambda g: (0, g)),
            pl.BlockSpec((rows, HEAD_DIM), lambda g: (0, local_heads + g)),
            pl.BlockSpec((tokens, HEAD_DIM), lambda g: (0, g)),
            pl.BlockSpec((tokens, HEAD_DIM), lambda g: (0, local_heads + g)),
            pl.BlockSpec((tokens, rows), lambda g: (0, 0)),
            pl.BlockSpec((tokens, tokens), lambda g: (0, 0)),
        ],
        out_specs=pl.BlockSpec((tokens, group_cols), lambda g: (0, g)),
        out_shape=jax.ShapeDtypeStruct((tokens, local_heads * group_cols), jnp.bfloat16),
        compiler_params=pltpu.CompilerParams(vmem_limit_bytes=48 * 1024 * 1024),
    )(queries, cache, cache, new_kv, new_kv, far_bias, near_bias)


def head_half(x, half, width):
    return lax.dynamic_slice_in_dim(x, half * width, width, axis=1)


def kv_half(x, half):
    kv_width = KV_HEADS * HEAD_DIM
    width = kv_width // 2
    return jnp.concatenate(
        [head_half(x[:, :kv_width], half, width), head_half(x[:, kv_width:], half, width)], axis=1
    )


def projection_kernel(a_ref, w_ref, o_ref):
    @pl.when(pl.program_id(0) == 0)
    def _():
        o_ref[...] = jnp.zeros_like(o_ref)

    part = jnp.dot(a_ref[...], w_ref[...], preferred_element_type=jnp.float32)
    o_ref[...] += part.astype(jnp.bfloat16).astype(jnp.float32)


def projection(attended, weight, group_rows):
    tokens = attended.shape[0]
    width = weight.shape[1]
    return pl.pallas_call(
        projection_kernel,
        grid=(weight.shape[0] // group_rows,),
        in_specs=[
            pl.BlockSpec((tokens, group_rows), lambda j: (0, j)),
            pl.BlockSpec((group_rows, width), lambda j: (j, 0)),
        ],
        out_specs=pl.BlockSpec((tokens, width), lambda j: (0, 0)),
        out_shape=jax.ShapeDtypeStruct((tokens, width), jnp.float32),
    )(attended, weight)


def expert_kernel(x_ref, wg_ref, wu_ref, wd_ref, o_ref):
    x = x_ref[...]
    gate = jnp.dot(x, wg_ref[...], preferred_element_type=jnp.float32)
    up = jnp.dot(x, wu_ref[...], preferred_element_type=jnp.float32)
    hidden = (gate / (1.0 + jnp.exp(-gate)) * up).astype(jnp.bfloat16)
    o_ref[...] = jnp.dot(hidden, wd_ref[...], preferred_element_type=jnp.float32).astype(o_ref.dtype)


def expert_ffn(stacked, gate_w, up_w, down_w, block_rows=256):
    rows, width = stacked.shape
    hidden = gate_w.shape[1]
    return pl.pallas_call(
        expert_kernel,
        grid=(rows // block_rows,),
        in_specs=[
            pl.BlockSpec((block_rows, width), lambda i: (i, 0)),
            pl.BlockSpec((width, hidden), lambda i: (0, 0)),
            pl.BlockSpec((width, hidden), lambda i: (0, 0)),
            pl.BlockSpec((hidden, width), lambda i: (0, 0)),
        ],
        out_specs=pl.BlockSpec((block_rows, width), lambda i: (i, 0)),
        out_shape=jax.ShapeDtypeStruct((rows, width), jnp.bfloat16),
        compiler_params=pltpu.CompilerParams(vmem_limit_bytes=48 * 1024 * 1024),
    )(stacked, gate_w, up_w, down_w)


def on_device(
    queries,
    new_kv,
    kv_cache,
    residual,
    token_request,
    request_leaf,
    mid_parent,
    leaf_parent,
    node_owner,
    node_len,
    out_weight,
    norm_gain,
    route_experts,
    route_weights,
    expert_gate,
    expert_up,
    expert_down,
):
    tokens_here = queries.shape[0]
    model_width = residual.shape[1]
    group_size = HEADS // KV_HEADS
    kv_width = KV_HEADS * HEAD_DIM
    head_scale = HEAD_DIM ** (-0.5)
    requests = token_request[0]
    ancestry = path_nodes(requests, request_leaf[0], mid_parent, leaf_parent)
    span_rows = kv_cache.shape[0]
    starts, finish = node_bounds(node_owner, node_len, span_rows)
    positions = jnp.arange(tokens_here, dtype=jnp.int32)
    own_mask = (requests[:, None] == requests[None, :]) & (positions[None, :] <= positions[:, None])
    core = lax.axis_index("core")
    other_core = 1 - core
    swap = [(0, 1), (1, 0)]
    cache_mine = lax.all_gather(kv_half(kv_cache, core), "gx", axis=0, tiled=True)
    cache_other = lax.ppermute(cache_mine, "core", swap)
    labels = key_labels(0, cache_mine.shape[0], starts, finish)
    seen_mask = jnp.any(labels[None, :, None] == ancestry[:, None, :], axis=2)
    far_bias = jnp.where(seen_mask, 0.0, -jnp.inf).astype(jnp.float32)
    near_bias = jnp.where(own_mask, 0.0, -jnp.inf).astype(jnp.float32)
    query_cols = queries.shape[1] // 2
    attended_mine = tree_attention(
        head_half(queries, core, query_cols), cache_mine, kv_half(new_kv, core), far_bias, near_bias
    )
    attended_other = tree_attention(
        head_half(queries, other_core, query_cols), cache_other, kv_half(new_kv, other_core), far_bias, near_bias
    )
    attended = jnp.where(
        core == 0,
        jnp.concatenate([attended_mine, attended_other], axis=1),
        jnp.concatenate([attended_other, attended_mine], axis=1),
    )
    shard_rows = out_weight.shape[0]
    shard_piece = lax.all_gather(out_weight, ("gyo", "core"), axis=0, tiled=True)
    projected = projection(attended, shard_piece, shard_rows)
    mixed_state = (residual.astype(jnp.float32) + projected).astype(jnp.bfloat16)
    mixed_float = lax.optimization_barrier(mixed_state).astype(jnp.float32)
    normed = (
        mixed_float
        * lax.rsqrt(jnp.mean(mixed_float * mixed_float, axis=1, keepdims=True) + EPSILON)
        * norm_gain
    ).astype(jnp.bfloat16)
    top_count = route_experts.shape[1]
    expert_count = lax.axis_size("gx") * lax.axis_size("gyo") * lax.axis_size("core") * expert_gate.shape[0]
    capacity = max(2, (3 * tokens_here * top_count + 2 * expert_count - 1) // (2 * expert_count))
    slots = -(-capacity // 16) * 16
    flat_experts = route_experts.reshape(-1)
    onehot = (flat_experts[:, None] == jnp.arange(expert_count, dtype=jnp.int32)[None, :]).astype(
        jnp.int32
    )
    slot_ids = jnp.sum((jnp.cumsum(onehot, axis=0) - onehot) * onehot, axis=1)
    target = (flat_experts * slots + slot_ids).reshape(tokens_here, top_count)
    row_range = jnp.arange(expert_count * slots, dtype=jnp.int32)
    pick = jnp.any(target[None, :, :] == row_range[:, None, None], axis=2).astype(jnp.bfloat16)
    weight_pick = jnp.sum(
        jnp.where(target[:, None, :] == row_range[None, :, None], route_weights[:, None, :], 0.0),
        axis=2,
    )
    outgoing = jnp.dot(pick, normed, preferred_element_type=jnp.float32).astype(jnp.bfloat16)
    outgoing = outgoing.reshape(expert_count, slots, model_width)
    arrived = lax.all_to_all(outgoing, TOKEN_AXES, split_axis=0, concat_axis=0, tiled=True)
    stacked = arrived.reshape(-1, model_width)
    expert_out = expert_ffn(stacked, expert_gate[0], expert_up[0], expert_down[0])
    returned = lax.all_to_all(
        expert_out.reshape(arrived.shape), TOKEN_AXES, split_axis=0, concat_axis=0, tiled=True
    )
    routed_sum = jnp.dot(
        weight_pick,
        returned.reshape(-1, model_width).astype(jnp.float32),
        precision=lax.Precision.HIGH,
        preferred_element_type=jnp.float32,
    )
    return (mixed_float + routed_sum).astype(jnp.bfloat16)

TOKEN_AXES = ("gx", "gyo", "core")


def solution(mesh):
    rows = P(TOKEN_AXES, None)
    split_mesh = jax.sharding.Mesh(
        mesh.devices.reshape(mesh.shape["gx"], mesh.shape["gy"] // 2, 2), TOKEN_AXES
    )
    in_specs = (
        rows,
        rows,
        P("gx", None),
        rows,
        rows,
        rows,
        P(),
        P(),
        P(),
        P(),
        P(("gyo", "core"), None),
        P(),
        rows,
        rows,
        P(TOKEN_AXES, None, None),
        P(TOKEN_AXES, None, None),
        P(TOKEN_AXES, None, None),
    )
    out_specs = rows
    return jax.shard_map(
        on_device, mesh=split_mesh, in_specs=in_specs, out_specs=out_specs, check_vma=False
    )
```

```python
import functools

import jax
import jax.numpy as jnp
from jax import lax
from jax.sharding import PartitionSpec as P
from jax.experimental import pallas as pl
from jax.experimental.pallas import tpu as pltpu

HEADS = 32
KV_HEADS = 4
HEAD_DIM = 128
ROOTS = 4
MIDS = 8


EPSILON = 1e-06


def node_bounds(node_owner, node_len, span_rows):
    labels = jnp.arange(node_owner.shape[0], dtype=jnp.int32)
    earlier = (node_owner[:, None] == node_owner[None, :]) & (labels[None, :] < labels[:, None])
    before = jnp.sum(jnp.where(earlier, node_len[None, :], 0), axis=1)
    starts = node_owner * span_rows + before
    return (starts, starts + node_len)


def key_labels(first_row, row_count, starts, finish):
    cache_rows = first_row + jnp.arange(row_count, dtype=jnp.int32)
    inside = (cache_rows[:, None] >= starts[None, :]) & (cache_rows[:, None] < finish[None, :])
    labels = jnp.arange(starts.shape[0], dtype=jnp.int32)
    return jnp.sum(jnp.where(inside, labels[None, :], 0), axis=1)


def path_nodes(requests, leaf_table, mid_parent, leaf_parent):
    picked = requests[:, None] == jnp.arange(leaf_table.shape[0], dtype=jnp.int32)[None, :]
    leaf_node = jnp.sum(jnp.where(picked, leaf_table[None, :], 0), axis=1)
    leaf_pick = leaf_node[:, None] == jnp.arange(leaf_parent.shape[0], dtype=jnp.int32)[None, :]
    middle_node = jnp.sum(jnp.where(leaf_pick, leaf_parent[None, :], 0), axis=1)
    middle_pick = middle_node[:, None] == jnp.arange(mid_parent.shape[0], dtype=jnp.int32)[None, :]
    root_node = jnp.sum(jnp.where(middle_pick, mid_parent[None, :], 0), axis=1)
    return jnp.stack([root_node, ROOTS + middle_node, ROOTS + MIDS + leaf_node], axis=1)


def masked_scores(query_heads, key_rows, allowed, head_scale):
    scores = (
        jnp.einsum("tgsd,kgd->gstk", query_heads, key_rows, preferred_element_type=jnp.float32)
        * head_scale
    )
    return jnp.where(allowed[None, None], scores, -jnp.inf)


def attention_kernel(q_ref, kc_ref, vc_ref, kn_ref, vn_ref, bf_ref, bn_ref, o_ref):
    head_scale = HEAD_DIM ** (-0.5)
    contract = (((1,), (1,)), ((), ()))
    far_keys = kc_ref[...]
    far_values = vc_ref[...]
    near_keys = kn_ref[...]
    near_values = vn_ref[...]
    far_bias = bf_ref[...]
    near_bias = bn_ref[...]
    for head in range(HEADS // KV_HEADS):
        cols = slice(head * HEAD_DIM, (head + 1) * HEAD_DIM)
        query = q_ref[:, cols]
        far = lax.dot_general(query, far_keys, contract, preferred_element_type=jnp.float32) + far_bias
        near = lax.dot_general(query, near_keys, contract, preferred_element_type=jnp.float32) + near_bias
        top = jnp.maximum(jnp.max(far, axis=1, keepdims=True), jnp.max(near, axis=1, keepdims=True))
        far_p = jnp.exp((far - top) * head_scale)
        near_p = jnp.exp((near - top) * head_scale)
        total = jnp.sum(far_p, axis=1, keepdims=True) + jnp.sum(near_p, axis=1, keepdims=True)
        summed = jnp.dot(
            far_p.astype(jnp.bfloat16), far_values, preferred_element_type=jnp.float32
        ) + jnp.dot(near_p.astype(jnp.bfloat16), near_values, preferred_element_type=jnp.float32)
        o_ref[:, cols] = (summed / total).astype(o_ref.dtype)


def tree_attention(queries, cache, new_kv, far_bias, near_bias):
    tokens = queries.shape[0]
    rows = cache.shape[0]
    group_cols = (HEADS // KV_HEADS) * HEAD_DIM
    local_heads = cache.shape[1] // (2 * HEAD_DIM)
    return pl.pallas_call(
        attention_kernel,
        grid=(local_heads,),
        in_specs=[
            pl.BlockSpec((tokens, group_cols), lambda g: (0, g)),
            pl.BlockSpec((rows, HEAD_DIM), lambda g: (0, g)),
            pl.BlockSpec((rows, HEAD_DIM), lambda g: (0, local_heads + g)),
            pl.BlockSpec((tokens, HEAD_DIM), lambda g: (0, g)),
            pl.BlockSpec((tokens, HEAD_DIM), lambda g: (0, local_heads + g)),
            pl.BlockSpec((tokens, rows), lambda g: (0, 0)),
            pl.BlockSpec((tokens, tokens), lambda g: (0, 0)),
        ],
        out_specs=pl.BlockSpec((tokens, group_cols), lambda g: (0, g)),
        out_shape=jax.ShapeDtypeStruct((tokens, local_heads * group_cols), jnp.bfloat16),
        compiler_params=pltpu.CompilerParams(vmem_limit_bytes=48 * 1024 * 1024),
    )(queries, cache, cache, new_kv, new_kv, far_bias, near_bias)


def head_half(x, half, width):
    return lax.dynamic_slice_in_dim(x, half * width, width, axis=1)


def kv_half(x, half):
    kv_width = KV_HEADS * HEAD_DIM
    width = kv_width // 2
    return jnp.concatenate(
        [head_half(x[:, :kv_width], half, width), head_half(x[:, kv_width:], half, width)], axis=1
    )


def projection_kernel(a_ref, w_ref, o_ref, *, group_rows):
    @pl.when(pl.program_id(0) == 0)
    def _():
        o_ref[...] = jnp.zeros_like(o_ref)

    total = o_ref[...]
    for group in range(w_ref.shape[0] // group_rows):
        rows = slice(group * group_rows, (group + 1) * group_rows)
        part = jnp.dot(a_ref[:, rows], w_ref[rows, :], preferred_element_type=jnp.float32)
        total = total + part.astype(jnp.bfloat16).astype(jnp.float32)
    o_ref[...] = total


def projection(attended, weight, group_rows, groups_per_step=4):
    tokens = attended.shape[0]
    width = weight.shape[1]
    step_rows = group_rows * groups_per_step
    return pl.pallas_call(
        functools.partial(projection_kernel, group_rows=group_rows),
        grid=(weight.shape[0] // step_rows,),
        in_specs=[
            pl.BlockSpec((tokens, step_rows), lambda j: (0, j)),
            pl.BlockSpec((step_rows, width), lambda j: (j, 0)),
        ],
        out_specs=pl.BlockSpec((tokens, width), lambda j: (0, 0)),
        out_shape=jax.ShapeDtypeStruct((tokens, width), jnp.float32),
        compiler_params=pltpu.CompilerParams(vmem_limit_bytes=48 * 1024 * 1024),
    )(attended, weight)

def expert_kernel(x_ref, wg_ref, wu_ref, wd_ref, o_ref):
    x = x_ref[...]
    gate = jnp.dot(x, wg_ref[...], preferred_element_type=jnp.float32)
    up = jnp.dot(x, wu_ref[...], preferred_element_type=jnp.float32)
    hidden = (gate / (1.0 + jnp.exp(-gate)) * up).astype(jnp.bfloat16)
    o_ref[...] = jnp.dot(hidden, wd_ref[...], preferred_element_type=jnp.float32).astype(o_ref.dtype)


def expert_ffn(stacked, gate_w, up_w, down_w, block_rows=512):
    rows, width = stacked.shape
    hidden = gate_w.shape[1]
    return pl.pallas_call(
        expert_kernel,
        grid=(rows // block_rows,),
        in_specs=[
            pl.BlockSpec((block_rows, width), lambda i: (i, 0)),
            pl.BlockSpec((width, hidden), lambda i: (0, 0)),
            pl.BlockSpec((width, hidden), lambda i: (0, 0)),
            pl.BlockSpec((hidden, width), lambda i: (0, 0)),
        ],
        out_specs=pl.BlockSpec((block_rows, width), lambda i: (i, 0)),
        out_shape=jax.ShapeDtypeStruct((rows, width), jnp.bfloat16),
        compiler_params=pltpu.CompilerParams(vmem_limit_bytes=48 * 1024 * 1024),
    )(stacked, gate_w, up_w, down_w)


def on_device(
    queries,
    new_kv,
    kv_cache,
    residual,
    token_request,
    request_leaf,
    mid_parent,
    leaf_parent,
    node_owner,
    node_len,
    out_weight,
    norm_gain,
    route_experts,
    route_weights,
    expert_gate,
    expert_up,
    expert_down,
):
    tokens_here = queries.shape[0]
    model_width = residual.shape[1]
    group_size = HEADS // KV_HEADS
    kv_width = KV_HEADS * HEAD_DIM
    head_scale = HEAD_DIM ** (-0.5)
    requests = token_request[0]
    ancestry = path_nodes(requests, request_leaf[0], mid_parent, leaf_parent)
    span_rows = kv_cache.shape[0]
    starts, finish = node_bounds(node_owner, node_len, span_rows)
    positions = jnp.arange(tokens_here, dtype=jnp.int32)
    own_mask = (requests[:, None] == requests[None, :]) & (positions[None, :] <= positions[:, None])
    core = lax.axis_index("core")
    other_core = 1 - core
    swap = [(0, 1), (1, 0)]
    cache_mine = lax.all_gather(kv_half(kv_cache, core), "gx", axis=0, tiled=True)
    cache_other = lax.ppermute(cache_mine, "core", swap)
    labels = key_labels(0, cache_mine.shape[0], starts, finish)
    seen_mask = jnp.any(labels[None, :, None] == ancestry[:, None, :], axis=2)
    far_bias = jnp.where(seen_mask, 0.0, -jnp.inf).astype(jnp.float32)
    near_bias = jnp.where(own_mask, 0.0, -jnp.inf).astype(jnp.float32)
    query_cols = queries.shape[1] // 2
    attended_mine = tree_attention(
        head_half(queries, core, query_cols), cache_mine, kv_half(new_kv, core), far_bias, near_bias
    )
    attended_other = tree_attention(
        head_half(queries, other_core, query_cols), cache_other, kv_half(new_kv, other_core), far_bias, near_bias
    )
    attended = jnp.where(
        core == 0,
        jnp.concatenate([attended_mine, attended_other], axis=1),
        jnp.concatenate([attended_other, attended_mine], axis=1),
    )
    shard_rows = out_weight.shape[0]
    shard_piece = lax.all_gather(out_weight, ("gyo", "core"), axis=0, tiled=True)
    projected = projection(attended, shard_piece, shard_rows)
    mixed_state = (residual.astype(jnp.float32) + projected).astype(jnp.bfloat16)
    mixed_float = lax.optimization_barrier(mixed_state).astype(jnp.float32)
    normed = (
        mixed_float
        * lax.rsqrt(jnp.mean(mixed_float * mixed_float, axis=1, keepdims=True) + EPSILON)
        * norm_gain
    ).astype(jnp.bfloat16)
    top_count = route_experts.shape[1]
    expert_count = lax.axis_size("gx") * lax.axis_size("gyo") * lax.axis_size("core") * expert_gate.shape[0]
    capacity = max(2, (3 * tokens_here * top_count + 2 * expert_count - 1) // (2 * expert_count))
    slots = -(-capacity // 16) * 16
    flat_experts = route_experts.reshape(-1)
    onehot = (flat_experts[:, None] == jnp.arange(expert_count, dtype=jnp.int32)[None, :]).astype(
        jnp.int32
    )
    slot_ids = jnp.sum((jnp.cumsum(onehot, axis=0) - onehot) * onehot, axis=1)
    target = (flat_experts * slots + slot_ids).reshape(tokens_here, top_count)
    row_range = jnp.arange(expert_count * slots, dtype=jnp.int32)
    pick = jnp.any(target[None, :, :] == row_range[:, None, None], axis=2).astype(jnp.bfloat16)
    weight_pick = jnp.sum(
        jnp.where(target[:, None, :] == row_range[None, :, None], route_weights[:, None, :], 0.0),
        axis=2,
    )
    outgoing = jnp.dot(pick, normed, preferred_element_type=jnp.float32).astype(jnp.bfloat16)
    outgoing = outgoing.reshape(expert_count, slots, model_width)
    arrived = lax.all_to_all(outgoing, TOKEN_AXES, split_axis=0, concat_axis=0, tiled=True)
    stacked = arrived.reshape(-1, model_width)
    expert_out = expert_ffn(stacked, expert_gate[0], expert_up[0], expert_down[0])
    returned = lax.all_to_all(
        expert_out.reshape(arrived.shape), TOKEN_AXES, split_axis=0, concat_axis=0, tiled=True
    )
    routed_sum = jnp.dot(
        weight_pick,
        returned.reshape(-1, model_width).astype(jnp.float32),
        precision=lax.Precision.HIGH,
        preferred_element_type=jnp.float32,
    )
    return (mixed_float + routed_sum).astype(jnp.bfloat16)

TOKEN_AXES = ("gx", "gyo", "core")


def solution(mesh):
    rows = P(TOKEN_AXES, None)
    split_mesh = jax.sharding.Mesh(
        mesh.devices.reshape(mesh.shape["gx"], mesh.shape["gy"] // 2, 2), TOKEN_AXES
    )
    in_specs = (
        rows,
        rows,
        P("gx", None),
        rows,
        rows,
        rows,
        P(),
        P(),
        P(),
        P(),
        P(("gyo", "core"), None),
        P(),
        rows,
        rows,
        P(TOKEN_AXES, None, None),
        P(TOKEN_AXES, None, None),
        P(TOKEN_AXES, None, None),
    )
    out_specs = rows
    return jax.shard_map(
        on_device, mesh=split_mesh, in_specs=in_specs, out_specs=out_specs, check_vma=False
    )
```

```python
import functools

import jax
import jax.numpy as jnp
from jax import lax
from jax.sharding import PartitionSpec as P
from jax.experimental import pallas as pl
from jax.experimental.pallas import tpu as pltpu

HEADS = 32
KV_HEADS = 4
HEAD_DIM = 128
ROOTS = 4
MIDS = 8


EPSILON = 1e-06


def node_bounds(node_owner, node_len, span_rows):
    labels = jnp.arange(node_owner.shape[0], dtype=jnp.int32)
    earlier = (node_owner[:, None] == node_owner[None, :]) & (labels[None, :] < labels[:, None])
    before = jnp.sum(jnp.where(earlier, node_len[None, :], 0), axis=1)
    starts = node_owner * span_rows + before
    return (starts, starts + node_len)


def key_labels(first_row, row_count, starts, finish):
    cache_rows = first_row + jnp.arange(row_count, dtype=jnp.int32)
    inside = (cache_rows[:, None] >= starts[None, :]) & (cache_rows[:, None] < finish[None, :])
    labels = jnp.arange(starts.shape[0], dtype=jnp.int32)
    return jnp.sum(jnp.where(inside, labels[None, :], 0), axis=1)


def path_nodes(requests, leaf_table, mid_parent, leaf_parent):
    picked = requests[:, None] == jnp.arange(leaf_table.shape[0], dtype=jnp.int32)[None, :]
    leaf_node = jnp.sum(jnp.where(picked, leaf_table[None, :], 0), axis=1)
    leaf_pick = leaf_node[:, None] == jnp.arange(leaf_parent.shape[0], dtype=jnp.int32)[None, :]
    middle_node = jnp.sum(jnp.where(leaf_pick, leaf_parent[None, :], 0), axis=1)
    middle_pick = middle_node[:, None] == jnp.arange(mid_parent.shape[0], dtype=jnp.int32)[None, :]
    root_node = jnp.sum(jnp.where(middle_pick, mid_parent[None, :], 0), axis=1)
    return jnp.stack([root_node, ROOTS + middle_node, ROOTS + MIDS + leaf_node], axis=1)


def masked_scores(query_heads, key_rows, allowed, head_scale):
    scores = (
        jnp.einsum("tgsd,kgd->gstk", query_heads, key_rows, preferred_element_type=jnp.float32)
        * head_scale
    )
    return jnp.where(allowed[None, None], scores, -jnp.inf)


def attention_kernel(q_ref, kc_ref, vc_ref, kn_ref, vn_ref, bf_ref, bn_ref, o_ref):
    head_scale = HEAD_DIM ** (-0.5)
    contract = (((1,), (1,)), ((), ()))
    far_keys = kc_ref[...]
    far_values = vc_ref[...]
    near_keys = kn_ref[...]
    near_values = vn_ref[...]
    far_bias = bf_ref[...]
    near_bias = bn_ref[...]
    for head in range(HEADS // KV_HEADS):
        cols = slice(head * HEAD_DIM, (head + 1) * HEAD_DIM)
        query = q_ref[:, cols]
        far = lax.dot_general(query, far_keys, contract, preferred_element_type=jnp.float32) + far_bias
        near = lax.dot_general(query, near_keys, contract, preferred_element_type=jnp.float32) + near_bias
        top = jnp.maximum(jnp.max(far, axis=1, keepdims=True), jnp.max(near, axis=1, keepdims=True))
        far_p = jnp.exp((far - top) * head_scale)
        near_p = jnp.exp((near - top) * head_scale)
        total = jnp.sum(far_p, axis=1, keepdims=True) + jnp.sum(near_p, axis=1, keepdims=True)
        summed = jnp.dot(
            far_p.astype(jnp.bfloat16), far_values, preferred_element_type=jnp.float32
        ) + jnp.dot(near_p.astype(jnp.bfloat16), near_values, preferred_element_type=jnp.float32)
        o_ref[:, cols] = (summed / total).astype(o_ref.dtype)


def tree_attention(queries, cache, new_kv, far_bias, near_bias):
    tokens = queries.shape[0]
    rows = cache.shape[0]
    group_cols = (HEADS // KV_HEADS) * HEAD_DIM
    local_heads = cache.shape[1] // (2 * HEAD_DIM)
    return pl.pallas_call(
        attention_kernel,
        grid=(local_heads,),
        in_specs=[
            pl.BlockSpec((tokens, group_cols), lambda g: (0, g)),
            pl.BlockSpec((rows, HEAD_DIM), lambda g: (0, g)),
            pl.BlockSpec((rows, HEAD_DIM), lambda g: (0, local_heads + g)),
            pl.BlockSpec((tokens, HEAD_DIM), lambda g: (0, g)),
            pl.BlockSpec((tokens, HEAD_DIM), lambda g: (0, local_heads + g)),
            pl.BlockSpec((tokens, rows), lambda g: (0, 0)),
            pl.BlockSpec((tokens, tokens), lambda g: (0, 0)),
        ],
        out_specs=pl.BlockSpec((tokens, group_cols), lambda g: (0, g)),
        out_shape=jax.ShapeDtypeStruct((tokens, local_heads * group_cols), jnp.bfloat16),
        compiler_params=pltpu.CompilerParams(vmem_limit_bytes=48 * 1024 * 1024),
    )(queries, cache, cache, new_kv, new_kv, far_bias, near_bias)


def head_half(x, half, width):
    return lax.dynamic_slice_in_dim(x, half * width, width, axis=1)


def kv_half(x, half):
    kv_width = KV_HEADS * HEAD_DIM
    width = kv_width // 2
    return jnp.concatenate(
        [head_half(x[:, :kv_width], half, width), head_half(x[:, kv_width:], half, width)], axis=1
    )


def projection_kernel(a_ref, w_ref, o_ref, *, group_rows):
    @pl.when(pl.program_id(0) == 0)
    def _():
        o_ref[...] = jnp.zeros_like(o_ref)

    total = o_ref[...]
    for group in range(w_ref.shape[0] // group_rows):
        rows = slice(group * group_rows, (group + 1) * group_rows)
        part = jnp.dot(a_ref[:, rows], w_ref[rows, :], preferred_element_type=jnp.float32)
        total = total + part.astype(jnp.bfloat16).astype(jnp.float32)
    o_ref[...] = total


def projection(attended, weight, group_rows, groups_per_step=4):
    tokens = attended.shape[0]
    width = weight.shape[1]
    step_rows = group_rows * groups_per_step
    return pl.pallas_call(
        functools.partial(projection_kernel, group_rows=group_rows),
        grid=(weight.shape[0] // step_rows,),
        in_specs=[
            pl.BlockSpec((tokens, step_rows), lambda j: (0, j)),
            pl.BlockSpec((step_rows, width), lambda j: (j, 0)),
        ],
        out_specs=pl.BlockSpec((tokens, width), lambda j: (0, 0)),
        out_shape=jax.ShapeDtypeStruct((tokens, width), jnp.float32),
        compiler_params=pltpu.CompilerParams(vmem_limit_bytes=48 * 1024 * 1024),
    )(attended, weight)

def expert_kernel(x_ref, wg_ref, wu_ref, wd_ref, o_ref):
    x = x_ref[...]
    gate = jnp.dot(x, wg_ref[...], preferred_element_type=jnp.float32)
    up = jnp.dot(x, wu_ref[...], preferred_element_type=jnp.float32)
    hidden = (gate / (1.0 + jnp.exp(-gate)) * up).astype(jnp.bfloat16)
    o_ref[...] = jnp.dot(hidden, wd_ref[...], preferred_element_type=jnp.float32).astype(o_ref.dtype)


def expert_ffn(stacked, gate_w, up_w, down_w, block_rows=512):
    rows, width = stacked.shape
    hidden = gate_w.shape[1]
    return pl.pallas_call(
        expert_kernel,
        grid=(rows // block_rows,),
        in_specs=[
            pl.BlockSpec((block_rows, width), lambda i: (i, 0)),
            pl.BlockSpec((width, hidden), lambda i: (0, 0)),
            pl.BlockSpec((width, hidden), lambda i: (0, 0)),
            pl.BlockSpec((hidden, width), lambda i: (0, 0)),
        ],
        out_specs=pl.BlockSpec((block_rows, width), lambda i: (i, 0)),
        out_shape=jax.ShapeDtypeStruct((rows, width), jnp.bfloat16),
        compiler_params=pltpu.CompilerParams(vmem_limit_bytes=48 * 1024 * 1024),
    )(stacked, gate_w, up_w, down_w)


def on_device(
    queries,
    new_kv,
    kv_cache,
    residual,
    token_request,
    request_leaf,
    mid_parent,
    leaf_parent,
    node_owner,
    node_len,
    out_weight,
    norm_gain,
    route_experts,
    route_weights,
    expert_gate,
    expert_up,
    expert_down,
):
    tokens_here = queries.shape[0]
    model_width = residual.shape[1]
    group_size = HEADS // KV_HEADS
    kv_width = KV_HEADS * HEAD_DIM
    head_scale = HEAD_DIM ** (-0.5)
    requests = token_request[0]
    ancestry = path_nodes(requests, request_leaf[0], mid_parent, leaf_parent)
    span_rows = kv_cache.shape[0]
    starts, finish = node_bounds(node_owner, node_len, span_rows)
    positions = jnp.arange(tokens_here, dtype=jnp.int32)
    own_mask = (requests[:, None] == requests[None, :]) & (positions[None, :] <= positions[:, None])
    core = lax.axis_index("core")
    other_core = 1 - core
    swap = [(0, 1), (1, 0)]
    cache_mine = lax.all_gather(kv_half(kv_cache, core), "gx", axis=0, tiled=True)
    cache_other = lax.ppermute(cache_mine, "core", swap)
    labels = key_labels(0, cache_mine.shape[0], starts, finish)
    seen_mask = jnp.any(labels[None, :, None] == ancestry[:, None, :], axis=2)
    far_bias = jnp.where(seen_mask, 0.0, -jnp.inf).astype(jnp.float32)
    near_bias = jnp.where(own_mask, 0.0, -jnp.inf).astype(jnp.float32)
    query_cols = queries.shape[1] // 2
    attended_mine = tree_attention(
        head_half(queries, core, query_cols), cache_mine, kv_half(new_kv, core), far_bias, near_bias
    )
    attended_other = tree_attention(
        head_half(queries, other_core, query_cols), cache_other, kv_half(new_kv, other_core), far_bias, near_bias
    )
    attended = jnp.where(
        core == 0,
        jnp.concatenate([attended_mine, attended_other], axis=1),
        jnp.concatenate([attended_other, attended_mine], axis=1),
    )
    shard_rows = out_weight.shape[0]
    shard_piece = lax.all_gather(out_weight, ("gyo", "core"), axis=0, tiled=True)
    projected = projection(attended, shard_piece, shard_rows)
    mixed_state = (residual.astype(jnp.float32) + projected).astype(jnp.bfloat16)
    mixed_float = lax.optimization_barrier(mixed_state).astype(jnp.float32)
    normed = (
        mixed_float
        * lax.rsqrt(jnp.mean(mixed_float * mixed_float, axis=1, keepdims=True) + EPSILON)
        * norm_gain
    ).astype(jnp.bfloat16)
    top_count = route_experts.shape[1]
    expert_count = lax.axis_size("gx") * lax.axis_size("gyo") * lax.axis_size("core") * expert_gate.shape[0]
    capacity = max(2, (3 * tokens_here * top_count + 2 * expert_count - 1) // (2 * expert_count))
    slots = -(-capacity // 16) * 16
    flat_experts = route_experts.reshape(-1)
    onehot = (flat_experts[:, None] == jnp.arange(expert_count, dtype=jnp.int32)[None, :]).astype(
        jnp.int32
    )
    slot_ids = jnp.sum((jnp.cumsum(onehot, axis=0) - onehot) * onehot, axis=1)
    target = (flat_experts * slots + slot_ids).reshape(tokens_here, top_count)
    row_range = jnp.arange(expert_count * slots, dtype=jnp.int32)
    pick = jnp.any(target[None, :, :] == row_range[:, None, None], axis=2).astype(jnp.bfloat16)
    weight_pick = jnp.sum(
        jnp.where(target[:, None, :] == row_range[None, :, None], route_weights[:, None, :], 0.0),
        axis=2,
    )
    outgoing = jnp.dot(pick, normed, preferred_element_type=jnp.float32).astype(jnp.bfloat16)
    outgoing = outgoing.reshape(expert_count, slots, model_width)
    arrived = lax.all_to_all(outgoing, TOKEN_AXES, split_axis=0, concat_axis=0, tiled=True)
    stacked = arrived.reshape(-1, model_width)
    expert_out = expert_ffn(stacked, expert_gate[0], expert_up[0], expert_down[0])
    returned = lax.all_to_all(
        expert_out.reshape(arrived.shape), TOKEN_AXES, split_axis=0, concat_axis=0, tiled=True
    )
    returned_rows = returned.reshape(-1, model_width)
    weight_high = weight_pick.astype(jnp.bfloat16)
    weight_low = (weight_pick - weight_high.astype(jnp.float32)).astype(jnp.bfloat16)
    routed_sum = jnp.dot(weight_high, returned_rows, preferred_element_type=jnp.float32) + jnp.dot(
        weight_low, returned_rows, preferred_element_type=jnp.float32
    )
    return (mixed_float + routed_sum).astype(jnp.bfloat16)

TOKEN_AXES = ("gx", "gyo", "core")


def solution(mesh):
    rows = P(TOKEN_AXES, None)
    split_mesh = jax.sharding.Mesh(
        mesh.devices.reshape(mesh.shape["gx"], mesh.shape["gy"] // 2, 2), TOKEN_AXES
    )
    in_specs = (
        rows,
        rows,
        P("gx", None),
        rows,
        rows,
        rows,
        P(),
        P(),
        P(),
        P(),
        P(("gyo", "core"), None),
        P(),
        rows,
        rows,
        P(TOKEN_AXES, None, None),
        P(TOKEN_AXES, None, None),
        P(TOKEN_AXES, None, None),
    )
    out_specs = rows
    return jax.shard_map(
        on_device, mesh=split_mesh, in_specs=in_specs, out_specs=out_specs, check_vma=False
    )
```

```python
import functools

import jax
import jax.numpy as jnp
from jax import lax
from jax.sharding import PartitionSpec as P
from jax.experimental import pallas as pl
from jax.experimental.pallas import tpu as pltpu

HEADS = 32
KV_HEADS = 4
HEAD_DIM = 128
ROOTS = 4
MIDS = 8


EPSILON = 1e-06


def node_bounds(node_owner, node_len, span_rows):
    labels = jnp.arange(node_owner.shape[0], dtype=jnp.int32)
    earlier = (node_owner[:, None] == node_owner[None, :]) & (labels[None, :] < labels[:, None])
    before = jnp.sum(jnp.where(earlier, node_len[None, :], 0), axis=1)
    starts = node_owner * span_rows + before
    return (starts, starts + node_len)


def key_labels(first_row, row_count, starts, finish):
    cache_rows = first_row + jnp.arange(row_count, dtype=jnp.int32)
    inside = (cache_rows[:, None] >= starts[None, :]) & (cache_rows[:, None] < finish[None, :])
    labels = jnp.arange(starts.shape[0], dtype=jnp.int32)
    return jnp.sum(jnp.where(inside, labels[None, :], 0), axis=1)


def path_nodes(requests, leaf_table, mid_parent, leaf_parent):
    picked = requests[:, None] == jnp.arange(leaf_table.shape[0], dtype=jnp.int32)[None, :]
    leaf_node = jnp.sum(jnp.where(picked, leaf_table[None, :], 0), axis=1)
    leaf_pick = leaf_node[:, None] == jnp.arange(leaf_parent.shape[0], dtype=jnp.int32)[None, :]
    middle_node = jnp.sum(jnp.where(leaf_pick, leaf_parent[None, :], 0), axis=1)
    middle_pick = middle_node[:, None] == jnp.arange(mid_parent.shape[0], dtype=jnp.int32)[None, :]
    root_node = jnp.sum(jnp.where(middle_pick, mid_parent[None, :], 0), axis=1)
    return jnp.stack([root_node, ROOTS + middle_node, ROOTS + MIDS + leaf_node], axis=1)


def masked_scores(query_heads, key_rows, allowed, head_scale):
    scores = (
        jnp.einsum("tgsd,kgd->gstk", query_heads, key_rows, preferred_element_type=jnp.float32)
        * head_scale
    )
    return jnp.where(allowed[None, None], scores, -jnp.inf)


def attention_kernel(q_ref, kc_ref, vc_ref, kn_ref, vn_ref, bf_ref, bn_ref, o_ref):
    head_scale = HEAD_DIM ** (-0.5)
    contract = (((1,), (1,)), ((), ()))
    far_keys = kc_ref[...]
    far_values = vc_ref[...]
    near_keys = kn_ref[...]
    near_values = vn_ref[...]
    far_bias = bf_ref[...]
    near_bias = bn_ref[...]
    for head in range(HEADS // KV_HEADS):
        cols = slice(head * HEAD_DIM, (head + 1) * HEAD_DIM)
        query = q_ref[:, cols]
        far = lax.dot_general(query, far_keys, contract, preferred_element_type=jnp.float32) + far_bias
        near = lax.dot_general(query, near_keys, contract, preferred_element_type=jnp.float32) + near_bias
        top = jnp.maximum(jnp.max(far, axis=1, keepdims=True), jnp.max(near, axis=1, keepdims=True))
        far_p = jnp.exp((far - top) * head_scale)
        near_p = jnp.exp((near - top) * head_scale)
        total = jnp.sum(far_p, axis=1, keepdims=True) + jnp.sum(near_p, axis=1, keepdims=True)
        summed = jnp.dot(
            far_p.astype(jnp.bfloat16), far_values, preferred_element_type=jnp.float32
        ) + jnp.dot(near_p.astype(jnp.bfloat16), near_values, preferred_element_type=jnp.float32)
        o_ref[:, cols] = (summed / total).astype(o_ref.dtype)


def tree_attention(queries, cache, new_kv, far_bias, near_bias):
    tokens = queries.shape[0]
    rows = cache.shape[0]
    group_cols = (HEADS // KV_HEADS) * HEAD_DIM
    local_heads = cache.shape[1] // (2 * HEAD_DIM)
    return pl.pallas_call(
        attention_kernel,
        grid=(local_heads,),
        in_specs=[
            pl.BlockSpec((tokens, group_cols), lambda g: (0, g)),
            pl.BlockSpec((rows, HEAD_DIM), lambda g: (0, g)),
            pl.BlockSpec((rows, HEAD_DIM), lambda g: (0, local_heads + g)),
            pl.BlockSpec((tokens, HEAD_DIM), lambda g: (0, g)),
            pl.BlockSpec((tokens, HEAD_DIM), lambda g: (0, local_heads + g)),
            pl.BlockSpec((tokens, rows), lambda g: (0, 0)),
            pl.BlockSpec((tokens, tokens), lambda g: (0, 0)),
        ],
        out_specs=pl.BlockSpec((tokens, group_cols), lambda g: (0, g)),
        out_shape=jax.ShapeDtypeStruct((tokens, local_heads * group_cols), jnp.bfloat16),
        compiler_params=pltpu.CompilerParams(vmem_limit_bytes=48 * 1024 * 1024),
    )(queries, cache, cache, new_kv, new_kv, far_bias, near_bias)


def head_half(x, half, width):
    return lax.dynamic_slice_in_dim(x, half * width, width, axis=1)


def kv_half(x, half):
    kv_width = KV_HEADS * HEAD_DIM
    width = kv_width // 2
    return jnp.concatenate(
        [head_half(x[:, :kv_width], half, width), head_half(x[:, kv_width:], half, width)], axis=1
    )


def projection_kernel(a_ref, w_ref, o_ref, *, group_rows):
    @pl.when(pl.program_id(0) == 0)
    def _():
        o_ref[...] = jnp.zeros_like(o_ref)

    total = o_ref[...]
    for group in range(w_ref.shape[0] // group_rows):
        rows = slice(group * group_rows, (group + 1) * group_rows)
        part = jnp.dot(a_ref[:, rows], w_ref[rows, :], preferred_element_type=jnp.float32)
        total = total + part.astype(jnp.bfloat16).astype(jnp.float32)
    o_ref[...] = total


def projection(attended, weight, group_rows, groups_per_step=8):
    tokens = attended.shape[0]
    width = weight.shape[1]
    step_rows = group_rows * groups_per_step
    return pl.pallas_call(
        functools.partial(projection_kernel, group_rows=group_rows),
        grid=(weight.shape[0] // step_rows,),
        in_specs=[
            pl.BlockSpec((tokens, step_rows), lambda j: (0, j)),
            pl.BlockSpec((step_rows, width), lambda j: (j, 0)),
        ],
        out_specs=pl.BlockSpec((tokens, width), lambda j: (0, 0)),
        out_shape=jax.ShapeDtypeStruct((tokens, width), jnp.float32),
        compiler_params=pltpu.CompilerParams(vmem_limit_bytes=48 * 1024 * 1024),
    )(attended, weight)

def expert_kernel(x_ref, wg_ref, wu_ref, wd_ref, o_ref):
    x = x_ref[...]
    gate = jnp.dot(x, wg_ref[...], preferred_element_type=jnp.float32)
    up = jnp.dot(x, wu_ref[...], preferred_element_type=jnp.float32)
    hidden = (gate / (1.0 + jnp.exp(-gate)) * up).astype(jnp.bfloat16)
    o_ref[...] = jnp.dot(hidden, wd_ref[...], preferred_element_type=jnp.float32).astype(o_ref.dtype)


def expert_ffn(stacked, gate_w, up_w, down_w, block_rows=512):
    rows, width = stacked.shape
    hidden = gate_w.shape[1]
    return pl.pallas_call(
        expert_kernel,
        grid=(rows // block_rows,),
        in_specs=[
            pl.BlockSpec((block_rows, width), lambda i: (i, 0)),
            pl.BlockSpec((width, hidden), lambda i: (0, 0)),
            pl.BlockSpec((width, hidden), lambda i: (0, 0)),
            pl.BlockSpec((hidden, width), lambda i: (0, 0)),
        ],
        out_specs=pl.BlockSpec((block_rows, width), lambda i: (i, 0)),
        out_shape=jax.ShapeDtypeStruct((rows, width), jnp.bfloat16),
        compiler_params=pltpu.CompilerParams(vmem_limit_bytes=48 * 1024 * 1024),
    )(stacked, gate_w, up_w, down_w)


def on_device(
    queries,
    new_kv,
    kv_cache,
    residual,
    token_request,
    request_leaf,
    mid_parent,
    leaf_parent,
    node_owner,
    node_len,
    out_weight,
    norm_gain,
    route_experts,
    route_weights,
    expert_gate,
    expert_up,
    expert_down,
):
    tokens_here = queries.shape[0]
    model_width = residual.shape[1]
    group_size = HEADS // KV_HEADS
    kv_width = KV_HEADS * HEAD_DIM
    head_scale = HEAD_DIM ** (-0.5)
    requests = token_request[0]
    ancestry = path_nodes(requests, request_leaf[0], mid_parent, leaf_parent)
    span_rows = kv_cache.shape[0]
    starts, finish = node_bounds(node_owner, node_len, span_rows)
    positions = jnp.arange(tokens_here, dtype=jnp.int32)
    own_mask = (requests[:, None] == requests[None, :]) & (positions[None, :] <= positions[:, None])
    core = lax.axis_index("core")
    other_core = 1 - core
    swap = [(0, 1), (1, 0)]
    cache_mine = lax.all_gather(kv_half(kv_cache, core), "gx", axis=0, tiled=True)
    cache_other = lax.ppermute(cache_mine, "core", swap)
    labels = key_labels(0, cache_mine.shape[0], starts, finish)
    seen_mask = jnp.any(labels[None, :, None] == ancestry[:, None, :], axis=2)
    far_bias = jnp.where(seen_mask, 0.0, -jnp.inf).astype(jnp.float32)
    near_bias = jnp.where(own_mask, 0.0, -jnp.inf).astype(jnp.float32)
    query_cols = queries.shape[1] // 2
    attended_mine = tree_attention(
        head_half(queries, core, query_cols), cache_mine, kv_half(new_kv, core), far_bias, near_bias
    )
    attended_other = tree_attention(
        head_half(queries, other_core, query_cols), cache_other, kv_half(new_kv, other_core), far_bias, near_bias
    )
    attended = jnp.where(
        core == 0,
        jnp.concatenate([attended_mine, attended_other], axis=1),
        jnp.concatenate([attended_other, attended_mine], axis=1),
    )
    shard_rows = out_weight.shape[0]
    shard_piece = lax.all_gather(out_weight, ("gyo", "core"), axis=0, tiled=True)
    projected = projection(attended, shard_piece, shard_rows)
    mixed_state = (residual.astype(jnp.float32) + projected).astype(jnp.bfloat16)
    mixed_float = lax.optimization_barrier(mixed_state).astype(jnp.float32)
    normed = (
        mixed_float
        * lax.rsqrt(jnp.mean(mixed_float * mixed_float, axis=1, keepdims=True) + EPSILON)
        * norm_gain
    ).astype(jnp.bfloat16)
    top_count = route_experts.shape[1]
    expert_count = lax.axis_size("gx") * lax.axis_size("gyo") * lax.axis_size("core") * expert_gate.shape[0]
    capacity = max(2, (3 * tokens_here * top_count + 2 * expert_count - 1) // (2 * expert_count))
    slots = -(-capacity // 16) * 16
    flat_experts = route_experts.reshape(-1)
    onehot = (flat_experts[:, None] == jnp.arange(expert_count, dtype=jnp.int32)[None, :]).astype(
        jnp.int32
    )
    slot_ids = jnp.sum((jnp.cumsum(onehot, axis=0) - onehot) * onehot, axis=1)
    target = (flat_experts * slots + slot_ids).reshape(tokens_here, top_count)
    row_range = jnp.arange(expert_count * slots, dtype=jnp.int32)
    pick = jnp.any(target[None, :, :] == row_range[:, None, None], axis=2).astype(jnp.bfloat16)
    weight_pick = jnp.sum(
        jnp.where(target[:, None, :] == row_range[None, :, None], route_weights[:, None, :], 0.0),
        axis=2,
    )
    outgoing = jnp.dot(pick, normed, preferred_element_type=jnp.float32).astype(jnp.bfloat16)
    outgoing = outgoing.reshape(expert_count, slots, model_width)
    arrived = lax.all_to_all(outgoing, TOKEN_AXES, split_axis=0, concat_axis=0, tiled=True)
    stacked = arrived.reshape(-1, model_width)
    expert_out = expert_ffn(stacked, expert_gate[0], expert_up[0], expert_down[0])
    returned = lax.all_to_all(
        expert_out.reshape(arrived.shape), TOKEN_AXES, split_axis=0, concat_axis=0, tiled=True
    )
    routed_sum = jnp.dot(
        weight_pick,
        returned.reshape(-1, model_width).astype(jnp.float32),
        precision=lax.Precision.HIGH,
        preferred_element_type=jnp.float32,
    )
    return (mixed_float + routed_sum).astype(jnp.bfloat16)

TOKEN_AXES = ("gx", "gyo", "core")


def solution(mesh):
    rows = P(TOKEN_AXES, None)
    split_mesh = jax.sharding.Mesh(
        mesh.devices.reshape(mesh.shape["gx"], mesh.shape["gy"] // 2, 2), TOKEN_AXES
    )
    in_specs = (
        rows,
        rows,
        P("gx", None),
        rows,
        rows,
        rows,
        P(),
        P(),
        P(),
        P(),
        P(("gyo", "core"), None),
        P(),
        rows,
        rows,
        P(TOKEN_AXES, None, None),
        P(TOKEN_AXES, None, None),
        P(TOKEN_AXES, None, None),
    )
    out_specs = rows
    return jax.shard_map(
        on_device, mesh=split_mesh, in_specs=in_specs, out_specs=out_specs, check_vma=False
    )
```
